128 devices in a mesh: row: 4 (over z_hi, core), col: 4 (over y), rep: 8 (over x, z_lo).
Axes of the slice: x: 4, y: 4, z: 4 (z_hi: 2, z_lo: 2; z = z_hi * 2 + z_lo), core: 2. Of those that a mesh axis runs over, the one named last changes fastest.
Arguments:
- hidden: bfloat16 [8, 2048, 2048], P('rep', ('row', 'col')), may hold values from -6 to 6
- lengths: int32 [8, 4], P('rep'), may hold values from 1 to 1536, 2048 in all within a row
- prefix_latent: bfloat16 [2048, 576], P(('row', 'col', 'rep')), may hold values from -6 to 6
- gain_in: bfloat16 [2048], replicated, may hold values from 0.25 to 1.75
- query_weight: bfloat16 [2048, 1536], replicated, may hold values from -0.125 to 0.125
- latent_down: bfloat16 [2048, 576], replicated, may hold values from -0.125 to 0.125
- latent_gain: bfloat16 [512], replicated, may hold values from 0.25 to 1.75
- key_absorb: bfloat16 [8, 128, 512], replicated, may hold values from -8 to 8
- value_up: bfloat16 [8, 512, 128], replicated, may hold values from -0.25 to 0.25
- output_weight: bfloat16 [1024, 2048], replicated, may hold values from -0.5 to 0.5
- post_gain: bfloat16 [2048], replicated, may hold values from 0.25 to 1.75
- routes: int32 [8, 2048, 6], P('rep', ('row', 'col')), may hold values from 0 to 63, all different within a row; in each aligned block of 128 rows (0 to 127, 128 to 255, ..., all dimensions but the last counted through in order) at most 16 rows name the same one
- gate_weights: float32 [8, 2048, 6], P('rep', ('row', 'col')), may hold values from 0.1 to 1
- expert_gate_up: bfloat16 [128, 2048, 1408], P(('row', 'col', 'rep')), may hold values from -0.125 to 0.125
- expert_down: bfloat16 [128, 704, 2048], P(('row', 'col', 'rep')), may hold values from -0.15625 to 0.15625
Outputs:
- attended: bfloat16 [8, 2048, 2048], P('rep', ('row', 'col'))
- layer_out: bfloat16 [8, 2048, 2048], P('rep', ('row', 'col'))
The draws below stay inside these ranges and needn't reach their ends.
Inputs may be any that keep to these rules, and one draw needn't show every extreme that they name: In each group the 4 lengths sum to 2048, and one of them is exactly 1536. `routes`: A token's 6 experts differ; among the 128 tokens of one device (aligned blocks of 128 tokens of a group) no expert is chosen more than 16 times, a bound that some block reaches.
All inputs are finite; a program needn't handle non-finite values.
Results may differ from the reference program's by a relative error of at most 0.014.
The reference program's roundings to bfloat16 on the way count: a program that leaves them out, or rounds other values in their place, can miss the bound.
Values may be sent and summed in bfloat16 or wider, within the bound.
No kernel may reach another device: no remote copies, remote signals or barrier semaphores. Data moves between devices by JAX's collectives and lax.ppermute only.
A program may use at most 128 MiB of HBM per device.

```python
import math
import jax
import jax.numpy as jnp
import numpy as np
from jax import lax

D = 2048
H = 8
NOPE = 128
ROPE = 64
RANK = 512
VD = 128
E = 64
TOP = 6
FF = 1408
FH = 704
REQS = 4
TOK_DEV = 128
TG = 2048
P_SIZE = 2048
CAP = 16
N_REP = 8


def draw_key_absorb(key, part):
    base = jax.random.normal(jax.random.fold_in(key, 11), (H, NOPE, RANK), jnp.float32)
    scale_value = 3.0 / math.sqrt(RANK)
    return jnp.clip(base * scale_value, -8.0, 8.0).astype(jnp.bfloat16)


def block_scale(own_key, shape, pieces, low, top_value):
    gain, own = 1.0, jax.random.fold_in(own_key, 6)
    for position, shards_of in pieces:
        steps = jnp.exp(jax.random.uniform(jax.random.fold_in(own, position), (shards_of,), jnp.float32, low / len(pieces), top_value / len(pieces)))
        gain = gain * jnp.repeat(steps, shape[position] // shards_of).reshape([-1 if axis == position else 1 for axis in range(len(shape))])
    return gain


def split_up(amount, total, most, lean):
    portions = [(1 << 20) // math.isqrt(standing ** lean) + 1 for standing in range(2, amount + 1)]
    spare, counts = total - most - (amount - 1), [1] * (amount - 1)
    while spare > 0:
        free = [i for i in range(amount - 1) if counts[i] < most]
        mass, remaining = sum([portions[i] for i in free]), spare
        for i in free:
            more = min(most - counts[i], max(1, remaining * portions[i] // mass), spare)
            counts[i] = counts[i] + more
            spare = spare - more
    return np.array([most] + counts)


def ragged_sizes(stream_key, amount, total, reach, slope):
    if amount == 2:
        one = jax.random.randint(stream_key, (), max(1, total - reach), min(reach, total - 1) + 1)
        return jnp.stack([one, total - one])
    tallies = jnp.asarray(split_up(amount, total, reach, slope), jnp.int32)
    twos = (amount - 1) // 2
    donor, sink = tallies[1:1 + 2 * twos:2], tallies[2:2 + 2 * twos:2]
    room = jnp.minimum(donor - 1, reach - sink)
    moved = jax.random.randint(jax.random.fold_in(stream_key, 1), (twos,), 0, 1 << 20) % (room + 1)
    tallies = tallies.at[1:1 + 2 * twos:2].set(donor - moved).at[2:2 + 2 * twos:2].set(sink + moved)
    return tallies[jax.random.permutation(jax.random.fold_in(stream_key, 2), amount)]


def shared_out(rng, own, number, rows, amount, top, reach, lean):
    sequence = jax.random.permutation(rng, amount)
    heavy_load, common = load_shares(amount, rows * top, reach, lean, True), load_shares(amount, rows * top, reach, lean, False)
    places = jnp.arange(amount)

    def named(tallies, offset_by):
        used = int((tallies > 0).sum())
        fixed = max(1, used // 4)
        shifted = fixed + (places - fixed + offset_by * (used - fixed)) % max(1, amount - fixed)
        return jnp.zeros((amount,), jnp.int32).at[sequence[jnp.where(places < fixed, places, shifted)]].set(jnp.asarray(tallies, jnp.int32))

    tallies = jnp.where(number % 4 == 0, named(heavy_load, number // 4), named(common, number - number // 4 - 1))
    mixed = jax.random.permutation(jax.random.fold_in(own, 3), amount)
    giver, taker = mixed[0:amount // 2 * 2:2], mixed[1:amount // 2 * 2:2]
    slack = jnp.minimum(tallies[giver] - 1, reach - tallies[taker]) // 2
    slack = jnp.where((giver == sequence[0]) | (taker == sequence[0]) | (tallies[taker] == 0), 0, jnp.maximum(slack, 0))
    shifted = jax.random.randint(jax.random.fold_in(own, 4), (amount // 2,), 0, 1 << 20) % (slack + 1)
    tallies = tallies.at[giver].add(-shifted).at[taker].add(shifted)
    labels = jnp.searchsorted(jnp.cumsum(tallies), jnp.arange(rows * top), side="right").astype(jnp.int32)
    grid = labels.reshape(top, rows).T
    grid = grid[jax.random.permutation(jax.random.fold_in(own, 1), rows)]
    offset_by = jax.random.randint(jax.random.fold_in(own, 2), (rows, 1), 0, top)
    return jnp.take_along_axis(grid, (jnp.arange(top)[None, :] + offset_by) % top, axis=1)


def load_shares(count, total, bound, lean, full):
    portions = [(1 << 20) // math.isqrt(rank ** lean) + 1 for rank in range(1, count + 1)]
    largest = bound if full else min(bound, max(-(-total // count), total * portions[0] // sum(portions)))
    least = 1 if total - largest >= count - 1 else 0
    counts, surplus = [largest] + [least] * (count - 1), total - largest - least * (count - 1)
    while surplus > 0:
        candidates = [i for i in range(1, count) if counts[i] < largest] or [i for i in range(1, count) if counts[i] < bound]
        whole, remaining = sum([portions[i] for i in candidates]), surplus
        for i in candidates:
            addition = min(bound - counts[i], max(1, remaining * portions[i] // whole), surplus)
            counts[i] = counts[i] + addition
            surplus = surplus - addition
    return np.array(counts)


def noise(stream_key, extent, width, bound, split=(), kind=jnp.bfloat16):
    values = jax.random.normal(stream_key, extent, jnp.float32) * width
    if len(split) > 0:
        values = block_scale(stream_key, extent, split, -0.22, 0.18) * values
    return jnp.clip(values, min=-bound, max=bound).astype(kind)


def setup_inputs(seed: int = 0) -> dict:
    streams_of = jax.random.split(jax.random.key(seed), 16)
    hidden = noise(streams_of[0], (N_REP, TG, D), 1.0, 6.0, ((0, 8), (1, 16)))
    lengths = jax.vmap(lambda own: ragged_sizes(own, REQS, TG, 3 * TG // 4, 2))(jax.random.split(streams_of[1], N_REP)).reshape((N_REP, REQS)).astype(jnp.int32)
    prefix_latent = noise(streams_of[2], (P_SIZE, RANK + ROPE), 1.0, 6.0, ((0, 128),))
    gain_in = jnp.clip(1.0 + 0.15 * jax.random.normal(streams_of[3], (D,), jnp.float32), 0.25, 1.75).astype(jnp.bfloat16)
    query_weight = noise(streams_of[4], (D, H * (NOPE + ROPE)), D ** -0.5, 0.125)
    latent_down = noise(streams_of[5], (D, RANK + ROPE), D ** -0.5, 0.125)
    latent_gain = jnp.clip(1.0 + 0.15 * jax.random.normal(streams_of[6], (RANK,), jnp.float32), 0.25, 1.75).astype(jnp.bfloat16)
    key_absorb = draw_key_absorb(jax.random.fold_in(streams_of[15], 71), 0)
    value_up = noise(streams_of[8], (H, RANK, VD), RANK ** -0.5, 0.25)
    output_weight = noise(streams_of[9], (H * VD, D), (H * VD // 8) ** -0.5, 0.5)
    post_gain = jnp.clip(1.0 + 0.15 * jax.random.normal(streams_of[10], (D,), jnp.float32), 0.25, 1.75).astype(jnp.bfloat16)
    routes_keys = jax.random.split(jax.random.fold_in(streams_of[11], 1), N_REP * TG // TOK_DEV)
    routes_turns = jax.random.permutation(jax.random.fold_in(streams_of[11], 3), N_REP * TG // TOK_DEV)
    routes = jax.vmap(lambda own, number: shared_out(jax.random.fold_in(streams_of[11], 2), own, number, TOK_DEV, E, TOP, CAP, 1))(routes_keys, routes_turns).reshape((N_REP, TG, TOP))
    gate_weights = jnp.clip(jnp.exp(math.log(1.0) - 2.3025851 * jax.random.uniform(streams_of[12], (N_REP, TG, TOP), jnp.float32) ** block_scale(streams_of[12], (N_REP, TG, TOP), ((0, 8), (1, 16)), -0.2, 0.2)), 0.1, 1.0)
    expert_gate_up = noise(streams_of[13], (2 * E, D, 2 * FH), D ** -0.5, 0.125, ((0, 128),))
    expert_down = noise(streams_of[14], (2 * E, FH, D), FF ** -0.5, 0.15625, ((0, 128),))
    return dict(hidden=hidden, lengths=lengths, prefix_latent=prefix_latent, gain_in=gain_in, query_weight=query_weight, latent_down=latent_down, latent_gain=latent_gain, key_absorb=key_absorb, value_up=value_up, output_weight=output_weight, post_gain=post_gain, routes=routes, gate_weights=gate_weights, expert_gate_up=expert_gate_up, expert_down=expert_down)


epsilon = 1e-06
rope_base = 50000.0

def rounded(values):
    return lax.optimization_barrier(values.astype(jnp.bfloat16))

def rms_scale(values, gain_vector):
    mean_square = lax.optimization_barrier(jnp.mean(values * values, axis=-1, keepdims=True))
    return values * lax.rsqrt(mean_square + epsilon) * gain_vector.astype(jnp.float32)

def rope_tables(positions, rope_width):
    halfway = rope_width // 2
    frequency = jnp.power(rope_base, -2.0 * jnp.arange(halfway, dtype=jnp.float32) / rope_width)
    angles = positions.astype(jnp.float32)[:, None] * frequency[None, :]
    return (jnp.cos(angles), jnp.sin(angles))

def rotate(values, cosine, sine_table):
    halfway = values.shape[-1] // 2
    leading = values[..., :halfway]
    trailing = values[..., halfway:]
    return jnp.concatenate([leading * cosine - trailing * sine_table, trailing * cosine + leading * sine_table], axis=-1)

def token_layout(group_lengths, first_place, row_count):
    ends = jnp.cumsum(group_lengths).astype(jnp.int32)
    starts = (ends - group_lengths).astype(jnp.int32)
    places = (first_place + jnp.arange(row_count, dtype=jnp.int32)).astype(jnp.int32)
    member = lax.optimization_barrier(jnp.sum((places[:, None] >= ends[None, :]).astype(jnp.int32), axis=1)).astype(jnp.int32)
    chosen = member[:, None] == jnp.arange(group_lengths.shape[0], dtype=jnp.int32)[None, :]
    offsets = lax.optimization_barrier(jnp.sum(jnp.where(chosen, starts[None, :], 0), axis=1)).astype(jnp.int32)
    return (member, places, (places - offsets).astype(jnp.int32))

def make_queries(normed, positions, query_weight, latent_down, latent_gain, key_absorb):
    row_count = normed.shape[0]
    head_count = key_absorb.shape[0]
    plain_width = key_absorb.shape[1]
    latent_width = latent_gain.shape[0]
    projected = jnp.dot(normed, query_weight, preferred_element_type=jnp.float32).reshape(row_count, head_count, -1)
    rope_width = projected.shape[-1] - plain_width
    cosine, sine_table = rope_tables(positions, rope_width)
    query_plain = rounded(projected[..., :plain_width]).astype(jnp.float32)
    query_rotary = rotate(projected[..., plain_width:], cosine[:, None, :], sine_table[:, None, :]).astype(jnp.bfloat16)
    query_latent = jnp.einsum('thn,hnr->thr', query_plain, key_absorb.astype(jnp.float32)).astype(jnp.bfloat16)
    query_rows = jnp.concatenate([query_latent, query_rotary], axis=-1)
    compressed = jnp.dot(normed, latent_down, preferred_element_type=jnp.float32)
    latent = rms_scale(compressed[:, :latent_width], latent_gain)
    key_rotary = rotate(compressed[:, latent_width:], cosine, sine_table)
    key_rows = jnp.concatenate([latent, key_rotary], axis=-1).astype(jnp.bfloat16)
    return (query_rows, key_rows)

def reference(hidden, lengths, prefix_latent, gain_in, query_weight, latent_down, latent_gain, key_absorb, value_up, output_weight, post_gain, routes, gate_weights, expert_gate_up, expert_down):
    scale_factor = 1.0 / math.sqrt(NOPE + ROPE)
    prefix_rows = prefix_latent.shape[0]

    def group_attention(inputs):
        group_hidden, group_lengths = inputs
        member, places, offsets = token_layout(group_lengths, 0, TG)
        normed = rms_scale(group_hidden.astype(jnp.float32), gain_in).astype(jnp.bfloat16)
        query_rows, key_rows = make_queries(normed, prefix_rows + offsets, query_weight, latent_down, latent_gain, key_absorb)
        all_keys = jnp.concatenate([prefix_latent, key_rows], axis=0)
        scores = jnp.einsum('thc,kc->thk', query_rows.astype(jnp.float32), all_keys.astype(jnp.float32)) * scale_factor
        allowed = (member[:, None] == member[None, :]) & (places[:, None] >= places[None, :])
        allowed = jnp.concatenate([jnp.ones((TG, prefix_rows), dtype=jnp.bool_), allowed], axis=1)
        scores = jnp.where(allowed[:, None, :], scores, -jnp.inf)
        peak = lax.optimization_barrier(jnp.max(scores, axis=2, keepdims=True))
        weights = jnp.exp(scores - peak)
        normalizer = lax.optimization_barrier(jnp.sum(weights, axis=2, keepdims=True))
        weights_low = rounded(weights).astype(jnp.float32)
        mixed = jnp.einsum('thk,kr->thr', weights_low, all_keys[:, :RANK].astype(jnp.float32)) / normalizer
        head_values = jnp.einsum('thr,hrv->thv', rounded(mixed).astype(jnp.float32), value_up.astype(jnp.float32))
        joined = head_values.astype(jnp.bfloat16).reshape(TG, -1)
        return jnp.dot(joined, output_weight, preferred_element_type=jnp.float32)
    attention = lax.map(group_attention, (hidden, lengths))
    tokens_all = N_REP * TG
    block_count = tokens_all // TOK_DEV
    residual = (hidden.astype(jnp.float32) + attention).astype(jnp.bfloat16).reshape(tokens_all, D)
    normed_post = rms_scale(residual.astype(jnp.float32), post_gain).astype(jnp.bfloat16)
    choices_flat = routes.reshape(block_count, TOK_DEV * TOP)
    gate_flat = gate_weights.reshape(block_count, TOK_DEV * TOP)
    selected = (choices_flat[:, :, None] == jnp.arange(E, dtype=jnp.int32)[None, None, :]).astype(jnp.int32)
    slot_index = (lax.optimization_barrier(jnp.sum(jnp.cumsum(selected, axis=1) * selected, axis=2)) - 1).astype(jnp.int32)
    block_index = jnp.broadcast_to(jnp.arange(block_count, dtype=jnp.int32)[:, None], choices_flat.shape)
    token_index = (block_index * TOK_DEV + jnp.arange(TOK_DEV * TOP, dtype=jnp.int32)[None, :] // TOP).astype(jnp.int32)
    slot_table = jnp.full((block_count, E, CAP), tokens_all, jnp.int32).at[block_index, choices_flat, slot_index].set(token_index)
    gate_table = jnp.zeros((block_count, E, CAP), jnp.float32).at[block_index, choices_flat, slot_index].set(gate_flat)
    slot_table = jnp.transpose(slot_table, (1, 0, 2)).reshape(E, block_count * CAP)
    gate_table = jnp.transpose(gate_table, (1, 0, 2)).reshape(E, block_count * CAP)
    padded = jnp.concatenate([normed_post, jnp.zeros((1, D), jnp.bfloat16)], axis=0)

    def expert_step(mixture, inputs):
        gate_up_pair, down_pair, row_index, row_gates = inputs
        token_rows = jnp.take(padded, row_index, axis=0)
        outputs = []
        for half_index in range(2):
            joint = jnp.dot(token_rows, gate_up_pair[half_index], preferred_element_type=jnp.float32)
            active = (jax.nn.silu(joint[:, :FH]) * joint[:, FH:]).astype(jnp.bfloat16)
            outputs.append(rounded(jnp.dot(active, down_pair[half_index], preferred_element_type=jnp.float32)).astype(jnp.float32))
        combined = (outputs[0] + outputs[1]) * row_gates[:, None]
        return (mixture.at[row_index].add(combined, mode='drop'), None)
    mixture = lax.scan(expert_step, jnp.zeros((tokens_all, D), jnp.float32), (expert_gate_up.reshape(E, 2, D, 2 * FH), expert_down.reshape(E, 2, FH, D), slot_table, gate_table))[0]
    layer_out = (residual.astype(jnp.float32) + mixture).astype(jnp.bfloat16).reshape(N_REP, TG, D)
    return (attention.astype(jnp.bfloat16), layer_out)
```

```python
import jax
import jax.numpy as jnp
from jax import lax
from jax.sharding import PartitionSpec as P

E = 64
CAP = 16


epsilon = 1e-06
rope_base = 50000.0
floor_value = -1e30


def rms_scale(values, gain_vector):
    mean_square = jnp.mean(values * values, axis=-1, keepdims=True)
    return values * lax.rsqrt(mean_square + epsilon) * gain_vector.astype(jnp.float32)


def rope_tables(positions, rope_width):
    halfway = rope_width // 2
    frequency = jnp.power(rope_base, -2.0 * jnp.arange(halfway, dtype=jnp.float32) / rope_width)
    angles = positions.astype(jnp.float32)[:, None] * frequency[None, :]
    return (jnp.cos(angles), jnp.sin(angles))


def rotate(values, cosine, sine_table):
    halfway = values.shape[-1] // 2
    leading = values[..., :halfway]
    trailing = values[..., halfway:]
    return jnp.concatenate(
        [leading * cosine - trailing * sine_table, trailing * cosine + leading * sine_table],
        axis=-1,
    )


def token_layout(group_lengths, first_place, row_count):
    ends = jnp.cumsum(group_lengths)
    starts = ends - group_lengths
    places = first_place + jnp.arange(row_count, dtype=jnp.int32)
    member = jnp.sum((places[:, None] >= ends[None, :]).astype(jnp.int32), axis=1)
    chosen = member[:, None] == jnp.arange(group_lengths.shape[0], dtype=jnp.int32)[None, :]
    offsets = jnp.sum(jnp.where(chosen, starts[None, :], 0), axis=1)
    return (member, places, places - offsets)


def make_queries(normed, positions, query_weight, latent_down, latent_gain, key_absorb):
    row_count = normed.shape[0]
    head_count = key_absorb.shape[0]
    plain_width = key_absorb.shape[1]
    latent_width = latent_gain.shape[0]
    projected = jnp.dot(normed, query_weight, preferred_element_type=jnp.float32).reshape(
        row_count, head_count, -1
    )
    rope_width = projected.shape[-1] - plain_width
    cosine, sine_table = rope_tables(positions, rope_width)
    query_plain = projected[..., :plain_width].astype(jnp.bfloat16)
    query_rotary = rotate(
        projected[..., plain_width:], cosine[:, None, :], sine_table[:, None, :]
    ).astype(jnp.bfloat16)
    query_latent = jnp.einsum(
        "thn,hnr->thr", query_plain, key_absorb, preferred_element_type=jnp.float32
    ).astype(jnp.bfloat16)
    query_rows = jnp.concatenate([query_latent, query_rotary], axis=-1)
    compressed = jnp.dot(normed, latent_down, preferred_element_type=jnp.float32)
    latent = rms_scale(compressed[:, :latent_width], latent_gain)
    key_rotary = rotate(compressed[:, latent_width:], cosine, sine_table)
    key_rows = jnp.concatenate([latent, key_rotary], axis=-1).astype(jnp.bfloat16)
    return (query_rows, key_rows)


def attend_block(state_now, query_rows, key_block, visible, scale_factor, latent_width):
    running_max, running_sum, weighted_sum = state_now
    scores = (
        lax.dot_general(
            query_rows, key_block, (((1,), (1,)), ((), ())), preferred_element_type=jnp.float32
        )
        * scale_factor
    )
    scores = jnp.where(visible, scores, -jnp.inf)
    new_max = jnp.maximum(running_max, jnp.max(scores, axis=1))
    rescale = jnp.exp(running_max - new_max)
    weights = jnp.exp(scores - new_max[:, None])
    running_sum = running_sum * rescale + jnp.sum(weights, axis=1)
    weighted_sum = weighted_sum * rescale[:, None] + jnp.dot(
        weights.astype(jnp.bfloat16),
        key_block[:, :latent_width],
        preferred_element_type=jnp.float32,
    )
    return (new_max, running_sum, weighted_sum)


def expert_apply(token_rows, expert_gate_up, expert_down):
    hidden_units = expert_down.shape[1]
    joint = jnp.einsum(
        "...hsd,hdf->...hsf", token_rows, expert_gate_up, preferred_element_type=jnp.float32
    )
    active = (jax.nn.silu(joint[..., :hidden_units]) * joint[..., hidden_units:]).astype(
        jnp.bfloat16
    )
    return jnp.einsum(
        "...hsf,hfd->...hsd", active, expert_down, preferred_element_type=jnp.float32
    ).astype(jnp.bfloat16)


def gather_rows(rows, axes):
    count = lax.axis_size(axes)
    copies = jnp.broadcast_to(rows[None], (count,) + rows.shape)
    gathered = lax.all_to_all(copies, axes, split_axis=0, concat_axis=0, tiled=True)
    return gathered.reshape(count * rows.shape[0], rows.shape[1])


def on_device(
    hidden,
    lengths,
    prefix_latent,
    gain_in,
    query_weight,
    latent_down,
    latent_gain,
    key_absorb,
    value_up,
    output_weight,
    post_gain,
    routes,
    gate_weights,
    expert_gate_up,
    expert_down,
):
    token_count = hidden.shape[1]
    model_width = hidden.shape[2]
    head_count = key_absorb.shape[0]
    latent_width = latent_gain.shape[0]
    scale_factor = float(query_weight.shape[1] // head_count) ** (-0.5)
    group_lengths = lengths[0]
    prefix_total = prefix_latent.shape[0] * lax.axis_size(("row", "col", "rep"))
    first_place = lax.axis_index(("row", "col")) * token_count
    member, places, offsets = token_layout(group_lengths, first_place, token_count)
    own_tokens = hidden[0]
    normed = rms_scale(own_tokens.astype(jnp.float32), gain_in).astype(jnp.bfloat16)
    query_rows, key_rows = make_queries(
        normed, prefix_total + offsets, query_weight, latent_down, latent_gain, key_absorb
    )
    query_rows = query_rows.reshape(token_count * head_count, -1)
    row_member = jnp.repeat(member, head_count)
    row_places = jnp.repeat(places, head_count)
    row_total = token_count * head_count
    initial = (
        jnp.full((row_total,), floor_value, jnp.float32),
        jnp.zeros((row_total,), jnp.float32),
        jnp.zeros((row_total, latent_width), jnp.float32),
    )
    after_prefix = attend_block(
        initial,
        query_rows,
        gather_rows(prefix_latent, ("row", "col", "rep")),
        True,
        scale_factor,
        latent_width,
    )
    key_block = lax.all_gather(key_rows, ("row", "col"), axis=0, tiled=True)
    block_member, block_places, block_offsets = token_layout(
        group_lengths, jnp.int32(0), key_block.shape[0]
    )
    visible = (row_member[:, None] == block_member[None, :]) & (
        row_places[:, None] >= block_places[None, :]
    )
    final_state = attend_block(
        after_prefix, query_rows, key_block, visible, scale_factor, latent_width
    )
    running_max, running_sum, weighted_sum = final_state
    mixed = (
        (weighted_sum / running_sum[:, None])
        .astype(jnp.bfloat16)
        .reshape(token_count, head_count, latent_width)
    )
    head_values = (
        jnp.einsum("thr,hrv->thv", mixed, value_up, preferred_element_type=jnp.float32)
        .astype(jnp.bfloat16)
        .reshape(token_count, -1)
    )
    attention = jnp.dot(head_values, output_weight, preferred_element_type=jnp.float32)
    residual = (own_tokens.astype(jnp.float32) + attention).astype(jnp.bfloat16)
    normed_post = rms_scale(residual.astype(jnp.float32), post_gain).astype(jnp.bfloat16)
    top_count = routes.shape[2]
    choices_flat = routes[0].reshape(-1)
    selected = (choices_flat[:, None] == jnp.arange(E, dtype=jnp.int32)[None, :]).astype(jnp.int32)
    slot_index = jnp.sum(jnp.cumsum(selected, axis=0) * selected, axis=1) - 1
    token_index = jnp.arange(choices_flat.shape[0], dtype=jnp.int32) // top_count
    slot_table = (
        jnp.full((E, CAP), token_count, jnp.int32).at[choices_flat, slot_index].set(token_index)
    )
    padded = jnp.concatenate([normed_post, jnp.zeros((1, model_width), jnp.bfloat16)], axis=0)
    gathered_rows = jnp.take(padded, slot_table.reshape(-1), axis=0).reshape(E, CAP, model_width)
    device_count = lax.axis_size(("row", "col", "rep"))
    per_device = expert_gate_up.shape[0]
    outgoing = jnp.broadcast_to(gathered_rows[:, None], (E, 2, CAP, model_width)).reshape(
        device_count, per_device, CAP, model_width
    )
    produced = expert_apply(
        lax.all_to_all(outgoing, ("row", "col", "rep"), split_axis=0, concat_axis=0, tiled=True),
        expert_gate_up,
        expert_down,
    )
    returned = lax.all_to_all(
        produced, ("row", "col", "rep"), split_axis=0, concat_axis=0, tiled=True
    )
    returned = returned.reshape(E, 2, CAP, model_width)
    paired = returned[:, 0].astype(jnp.float32) + returned[:, 1].astype(jnp.float32)
    picked = jnp.take(
        paired.reshape(E * CAP, model_width), choices_flat * CAP + slot_index, axis=0
    ).reshape(token_count, top_count, model_width)
    mixture = jnp.sum(picked * gate_weights[0][:, :, None], axis=1)
    layer_out = (residual.astype(jnp.float32) + mixture).astype(jnp.bfloat16)
    return (attention.astype(jnp.bfloat16)[None], layer_out[None])


def solution(mesh):
    in_specs = (
        P("rep", ("row", "col"), None),
        P("rep", None),
        P(("row", "col", "rep"), None),
        P(),
        P(),
        P(),
        P(),
        P(),
        P(),
        P(),
        P(),
        P("rep", ("row", "col"), None),
        P("rep", ("row", "col"), None),
        P(("row", "col", "rep"), None, None),
        P(("row", "col", "rep"), None, None),
    )
    out_specs = (P("rep", ("row", "col"), None), P("rep", ("row", "col"), None))
    return jax.shard_map(
        on_device, mesh=mesh, in_specs=in_specs, out_specs=out_specs, check_vma=False
    )
```

```python
import jax
import jax.numpy as jnp
from jax import lax
from jax.sharding import PartitionSpec as P

E = 64
CAP = 16


epsilon = 1e-06
rope_base = 50000.0
floor_value = -1e30


def rms_scale(values, gain_vector):
    mean_square = jnp.mean(values * values, axis=-1, keepdims=True)
    return values * lax.rsqrt(mean_square + epsilon) * gain_vector.astype(jnp.float32)


def rope_tables(positions, rope_width):
    halfway = rope_width // 2
    frequency = jnp.power(rope_base, -2.0 * jnp.arange(halfway, dtype=jnp.float32) / rope_width)
    angles = positions.astype(jnp.float32)[:, None] * frequency[None, :]
    return (jnp.cos(angles), jnp.sin(angles))


def rotate(values, cosine, sine_table):
    halfway = values.shape[-1] // 2
    leading = values[..., :halfway]
    trailing = values[..., halfway:]
    return jnp.concatenate(
        [leading * cosine - trailing * sine_table, trailing * cosine + leading * sine_table],
        axis=-1,
    )


def token_layout(group_lengths, first_place, row_count):
    ends = jnp.cumsum(group_lengths)
    starts = ends - group_lengths
    places = first_place + jnp.arange(row_count, dtype=jnp.int32)
    member = jnp.sum((places[:, None] >= ends[None, :]).astype(jnp.int32), axis=1)
    chosen = member[:, None] == jnp.arange(group_lengths.shape[0], dtype=jnp.int32)[None, :]
    offsets = jnp.sum(jnp.where(chosen, starts[None, :], 0), axis=1)
    return (member, places, places - offsets)


def make_queries(normed, positions, query_weight, latent_down, latent_gain, key_absorb):
    row_count = normed.shape[0]
    head_count = key_absorb.shape[0]
    plain_width = key_absorb.shape[1]
    latent_width = latent_gain.shape[0]
    projected = jnp.dot(normed, query_weight, preferred_element_type=jnp.float32).reshape(
        row_count, head_count, -1
    )
    rope_width = projected.shape[-1] - plain_width
    cosine, sine_table = rope_tables(positions, rope_width)
    query_plain = projected[..., :plain_width].astype(jnp.bfloat16)
    query_rotary = rotate(
        projected[..., plain_width:], cosine[:, None, :], sine_table[:, None, :]
    ).astype(jnp.bfloat16)
    query_latent = jnp.einsum(
        "thn,hnr->thr", query_plain, key_absorb, preferred_element_type=jnp.float32
    ).astype(jnp.bfloat16)
    query_rows = jnp.concatenate([query_latent, query_rotary], axis=-1)
    compressed = jnp.dot(normed, latent_down, preferred_element_type=jnp.float32)
    latent = rms_scale(compressed[:, :latent_width], latent_gain)
    key_rotary = rotate(compressed[:, latent_width:], cosine, sine_table)
    key_rows = jnp.concatenate([latent, key_rotary], axis=-1).astype(jnp.bfloat16)
    return (query_rows, key_rows)


def attend_block(state_now, query_rows, key_block, visible, scale_factor, latent_width):
    running_max, running_sum, weighted_sum = state_now
    scores = (
        lax.dot_general(
            query_rows, key_block, (((1,), (1,)), ((), ())), preferred_element_type=jnp.float32
        )
        * scale_factor
    )
    scores = jnp.where(visible, scores, -jnp.inf)
    new_max = jnp.maximum(running_max, jnp.max(scores, axis=1))
    rescale = jnp.exp(running_max - new_max)
    weights = jnp.exp(scores - new_max[:, None])
    running_sum = running_sum * rescale + jnp.sum(weights, axis=1)
    weighted_sum = weighted_sum * rescale[:, None] + jnp.dot(
        weights.astype(jnp.bfloat16),
        key_block[:, :latent_width],
        preferred_element_type=jnp.float32,
    )
    return (new_max, running_sum, weighted_sum)


def expert_apply(token_rows, expert_gate_up, expert_down):
    hidden_units = expert_down.shape[1]
    joint = jnp.einsum(
        "...hsd,hdf->...hsf", token_rows, expert_gate_up, preferred_element_type=jnp.float32
    )
    active = (jax.nn.silu(joint[..., :hidden_units]) * joint[..., hidden_units:]).astype(
        jnp.bfloat16
    )
    return jnp.einsum(
        "...hsf,hfd->...hsd", active, expert_down, preferred_element_type=jnp.float32
    ).astype(jnp.bfloat16)


def gather_rows(rows, axes):
    count = lax.axis_size(axes)
    copies = jnp.broadcast_to(rows[None], (count,) + rows.shape)
    gathered = lax.all_to_all(copies, axes, split_axis=0, concat_axis=0, tiled=True)
    return gathered.reshape(count * rows.shape[0], rows.shape[1])


def on_device(
    hidden,
    lengths,
    prefix_latent,
    gain_in,
    query_weight,
    latent_down,
    latent_gain,
    key_absorb,
    value_up,
    output_weight,
    post_gain,
    routes,
    gate_weights,
    expert_gate_up,
    expert_down,
):
    token_count = hidden.shape[1]
    model_width = hidden.shape[2]
    head_count = key_absorb.shape[0]
    latent_width = latent_gain.shape[0]
    scale_factor = float(query_weight.shape[1] // head_count) ** (-0.5)
    group_lengths = lengths[0]
    prefix_total = prefix_latent.shape[0] * lax.axis_size(("row", "col", "rep"))
    first_place = lax.axis_index(("row", "col")) * token_count
    member, places, offsets = token_layout(group_lengths, first_place, token_count)
    own_tokens = hidden[0]
    normed = rms_scale(own_tokens.astype(jnp.float32), gain_in).astype(jnp.bfloat16)
    query_rows, key_rows = make_queries(
        normed, prefix_total + offsets, query_weight, latent_down, latent_gain, key_absorb
    )
    query_rows = query_rows.reshape(token_count * head_count, -1)
    row_member = jnp.repeat(member, head_count)
    row_places = jnp.repeat(places, head_count)
    row_total = token_count * head_count
    initial = (
        jnp.full((row_total,), floor_value, jnp.float32),
        jnp.zeros((row_total,), jnp.float32),
        jnp.zeros((row_total, latent_width), jnp.float32),
    )
    after_prefix = attend_block(
        initial,
        query_rows,
        gather_rows(prefix_latent, ("row", "col", "rep")),
        True,
        scale_factor,
        latent_width,
    )
    key_block = lax.all_gather(key_rows, ("row", "col"), axis=0, tiled=True)
    block_member, block_places, block_offsets = token_layout(
        group_lengths, jnp.int32(0), key_block.shape[0]
    )
    visible = (row_member[:, None] == block_member[None, :]) & (
        row_places[:, None] >= block_places[None, :]
    )
    final_state = attend_block(
        after_prefix, query_rows, key_block, visible, scale_factor, latent_width
    )
    running_max, running_sum, weighted_sum = final_state
    mixed = (
        (weighted_sum / running_sum[:, None])
        .astype(jnp.bfloat16)
        .reshape(token_count, head_count, latent_width)
    )
    head_values = (
        jnp.einsum("thr,hrv->thv", mixed, value_up, preferred_element_type=jnp.float32)
        .astype(jnp.bfloat16)
        .reshape(token_count, -1)
    )
    attention = jnp.dot(head_values, output_weight, preferred_element_type=jnp.float32)
    residual = (own_tokens.astype(jnp.float32) + attention).astype(jnp.bfloat16)
    normed_post = rms_scale(residual.astype(jnp.float32), post_gain).astype(jnp.bfloat16)
    top_count = routes.shape[2]
    pair_count = token_count * top_count
    choices_flat = routes[0].reshape(-1)
    selected = (choices_flat[:, None] == jnp.arange(E, dtype=jnp.int32)[None, :]).astype(
        jnp.bfloat16
    )
    pair_ids = jnp.arange(pair_count, dtype=jnp.int32)
    lower = (pair_ids[:, None] >= pair_ids[None, :]).astype(jnp.bfloat16)
    running = jnp.dot(lower, selected, preferred_element_type=jnp.float32)
    slot_index = (
        jnp.sum(running * selected.astype(jnp.float32), axis=1).astype(jnp.int32) - 1
    )
    slot_place = choices_flat * CAP + slot_index
    pick_table = (
        slot_place[:, None] == jnp.arange(E * CAP, dtype=jnp.int32)[None, :]
    ).astype(jnp.bfloat16).reshape(token_count, top_count, E * CAP)
    occupancy = jnp.sum(pick_table, axis=1).reshape(token_count, E, 1, CAP)
    send_table = jnp.broadcast_to(occupancy, (token_count, E, 2, CAP)).reshape(token_count, -1)
    device_count = lax.axis_size(("row", "col", "rep"))
    per_device = expert_gate_up.shape[0]
    outgoing = (
        jnp.einsum("tj,td->jd", send_table, normed_post, preferred_element_type=jnp.float32)
        .astype(jnp.bfloat16)
        .reshape(device_count, per_device, CAP, model_width)
    )
    produced = expert_apply(
        lax.all_to_all(outgoing, ("row", "col", "rep"), split_axis=0, concat_axis=0, tiled=True),
        expert_gate_up,
        expert_down,
    )
    returned = lax.all_to_all(
        produced, ("row", "col", "rep"), split_axis=0, concat_axis=0, tiled=True
    )
    returned = returned.reshape(E, 2, CAP, model_width)
    picked_first = jnp.einsum(
        "tkp,pd->tkd",
        pick_table,
        returned[:, 0].reshape(E * CAP, model_width),
        preferred_element_type=jnp.float32,
    )
    picked_second = jnp.einsum(
        "tkp,pd->tkd",
        pick_table,
        returned[:, 1].reshape(E * CAP, model_width),
        preferred_element_type=jnp.float32,
    )
    picked = picked_first + picked_second
    mixture = jnp.sum(picked * gate_weights[0][:, :, None], axis=1)
    layer_out = (residual.astype(jnp.float32) + mixture).astype(jnp.bfloat16)
    return (attention.astype(jnp.bfloat16)[None], layer_out[None])


def solution(mesh):
    in_specs = (
        P("rep", ("row", "col"), None),
        P("rep", None),
        P(("row", "col", "rep"), None),
        P(),
        P(),
        P(),
        P(),
        P(),
        P(),
        P(),
        P(),
        P("rep", ("row", "col"), None),
        P("rep", ("row", "col"), None),
        P(("row", "col", "rep"), None, None),
        P(("row", "col", "rep"), None, None),
    )
    out_specs = (P("rep", ("row", "col"), None), P("rep", ("row", "col"), None))
    return jax.shard_map(
        on_device, mesh=mesh, in_specs=in_specs, out_specs=out_specs, check_vma=False
    )
```

```python
import jax
import jax.numpy as jnp
from jax import lax
from jax.sharding import PartitionSpec as P

E = 64
CAP = 16


epsilon = 1e-06
rope_base = 50000.0
floor_value = -1e30


def rms_scale(values, gain_vector):
    mean_square = jnp.mean(values * values, axis=-1, keepdims=True)
    return values * lax.rsqrt(mean_square + epsilon) * gain_vector.astype(jnp.float32)


def rope_tables(positions, rope_width):
    halfway = rope_width // 2
    frequency = jnp.power(rope_base, -2.0 * jnp.arange(halfway, dtype=jnp.float32) / rope_width)
    angles = positions.astype(jnp.float32)[:, None] * frequency[None, :]
    return (jnp.cos(angles), jnp.sin(angles))


def rotate(values, cosine, sine_table):
    halfway = values.shape[-1] // 2
    leading = values[..., :halfway]
    trailing = values[..., halfway:]
    return jnp.concatenate(
        [leading * cosine - trailing * sine_table, trailing * cosine + leading * sine_table],
        axis=-1,
    )


def token_layout(group_lengths, first_place, row_count):
    ends = jnp.cumsum(group_lengths)
    starts = ends - group_lengths
    places = first_place + jnp.arange(row_count, dtype=jnp.int32)
    member = jnp.sum((places[:, None] >= ends[None, :]).astype(jnp.int32), axis=1)
    chosen = member[:, None] == jnp.arange(group_lengths.shape[0], dtype=jnp.int32)[None, :]
    offsets = jnp.sum(jnp.where(chosen, starts[None, :], 0), axis=1)
    return (member, places, places - offsets)


def make_queries(normed, positions, query_weight, latent_down, latent_gain, key_absorb):
    row_count = normed.shape[0]
    head_count = key_absorb.shape[0]
    plain_width = key_absorb.shape[1]
    latent_width = latent_gain.shape[0]
    projected = jnp.dot(normed, query_weight, preferred_element_type=jnp.float32).reshape(
        row_count, head_count, -1
    )
    rope_width = projected.shape[-1] - plain_width
    cosine, sine_table = rope_tables(positions, rope_width)
    query_plain = projected[..., :plain_width].astype(jnp.bfloat16)
    query_rotary = rotate(
        projected[..., plain_width:], cosine[:, None, :], sine_table[:, None, :]
    ).astype(jnp.bfloat16)
    query_latent = jnp.einsum(
        "thn,hnr->thr", query_plain, key_absorb, preferred_element_type=jnp.float32
    ).astype(jnp.bfloat16)
    query_rows = jnp.concatenate([query_latent, query_rotary], axis=-1)
    compressed = jnp.dot(normed, latent_down, preferred_element_type=jnp.float32)
    latent = rms_scale(compressed[:, :latent_width], latent_gain)
    key_rotary = rotate(compressed[:, latent_width:], cosine, sine_table)
    key_rows = jnp.concatenate([latent, key_rotary], axis=-1).astype(jnp.bfloat16)
    return (query_rows, key_rows)


def attend_block(state_now, query_rows, key_block, visible, scale_factor, latent_width):
    running_max, running_sum, weighted_sum = state_now
    scores = (
        lax.dot_general(
            query_rows, key_block, (((1,), (1,)), ((), ())), preferred_element_type=jnp.float32
        )
        * scale_factor
    )
    scores = jnp.where(visible, scores, -jnp.inf)
    new_max = jnp.maximum(running_max, jnp.max(scores, axis=1))
    rescale = jnp.exp(running_max - new_max)
    weights = jnp.exp(scores - new_max[:, None])
    running_sum = running_sum * rescale + jnp.sum(weights, axis=1)
    weighted_sum = weighted_sum * rescale[:, None] + jnp.dot(
        weights.astype(jnp.bfloat16),
        key_block[:, :latent_width],
        preferred_element_type=jnp.float32,
    )
    return (new_max, running_sum, weighted_sum)


def expert_apply(token_rows, expert_gate_up, expert_down):
    hidden_units = expert_down.shape[1]
    rows = token_rows.reshape(-1, token_rows.shape[-1])
    joint = jnp.dot(rows, expert_gate_up[0], preferred_element_type=jnp.float32)
    active = (jax.nn.silu(joint[:, :hidden_units]) * joint[:, hidden_units:]).astype(jnp.bfloat16)
    produced = jnp.dot(active, expert_down[0], preferred_element_type=jnp.float32)
    return produced.astype(jnp.bfloat16).reshape(token_rows.shape)


def gather_rows(rows, axes):
    count = lax.axis_size(axes)
    copies = jnp.broadcast_to(rows[None], (count,) + rows.shape)
    gathered = lax.all_to_all(copies, axes, split_axis=0, concat_axis=0, tiled=True)
    return gathered.reshape(count * rows.shape[0], rows.shape[1])


def on_device(
    hidden,
    lengths,
    prefix_latent,
    gain_in,
    query_weight,
    latent_down,
    latent_gain,
    key_absorb,
    value_up,
    output_weight,
    post_gain,
    routes,
    gate_weights,
    expert_gate_up,
    expert_down,
):
    token_count = hidden.shape[1]
    model_width = hidden.shape[2]
    head_count = key_absorb.shape[0]
    latent_width = latent_gain.shape[0]
    scale_factor = float(query_weight.shape[1] // head_count) ** (-0.5)
    group_lengths = lengths[0]
    prefix_total = prefix_latent.shape[0] * lax.axis_size(("row", "col", "rep"))
    first_place = lax.axis_index(("row", "col")) * token_count
    member, places, offsets = token_layout(group_lengths, first_place, token_count)
    own_tokens = hidden[0]
    normed = rms_scale(own_tokens.astype(jnp.float32), gain_in).astype(jnp.bfloat16)
    query_rows, key_rows = make_queries(
        normed, prefix_total + offsets, query_weight, latent_down, latent_gain, key_absorb
    )
    query_rows = query_rows.reshape(token_count * head_count, -1)
    row_member = jnp.repeat(member, head_count)
    row_places = jnp.repeat(places, head_count)
    row_total = token_count * head_count
    initial = (
        jnp.full((row_total,), floor_value, jnp.float32),
        jnp.zeros((row_total,), jnp.float32),
        jnp.zeros((row_total, latent_width), jnp.float32),
    )
    after_prefix = attend_block(
        initial,
        query_rows,
        gather_rows(prefix_latent, ("row", "col", "rep")),
        True,
        scale_factor,
        latent_width,
    )
    key_block = lax.all_gather(
        lax.all_gather(key_rows, "col", axis=0, tiled=True), "row", axis=0, tiled=True
    )
    block_member, block_places, block_offsets = token_layout(
        group_lengths, jnp.int32(0), key_block.shape[0]
    )
    visible = (row_member[:, None] == block_member[None, :]) & (
        row_places[:, None] >= block_places[None, :]
    )
    final_state = attend_block(
        after_prefix, query_rows, key_block, visible, scale_factor, latent_width
    )
    running_max, running_sum, weighted_sum = final_state
    mixed = (
        (weighted_sum / running_sum[:, None])
        .astype(jnp.bfloat16)
        .reshape(token_count, head_count, latent_width)
    )
    head_values = (
        jnp.einsum("thr,hrv->thv", mixed, value_up, preferred_element_type=jnp.float32)
        .astype(jnp.bfloat16)
        .reshape(token_count, -1)
    )
    attention = jnp.dot(head_values, output_weight, preferred_element_type=jnp.float32)
    residual = (own_tokens.astype(jnp.float32) + attention).astype(jnp.bfloat16)
    normed_post = rms_scale(residual.astype(jnp.float32), post_gain).astype(jnp.bfloat16)
    top_count = routes.shape[2]
    pair_count = token_count * top_count
    choices_flat = routes[0].reshape(-1)
    selected = (choices_flat[:, None] == jnp.arange(E, dtype=jnp.int32)[None, :]).astype(
        jnp.bfloat16
    )
    pair_ids = jnp.arange(pair_count, dtype=jnp.int32)
    lower = (pair_ids[:, None] >= pair_ids[None, :]).astype(jnp.bfloat16)
    running = jnp.dot(lower, selected, preferred_element_type=jnp.float32)
    slot_index = (
        jnp.sum(running * selected.astype(jnp.float32), axis=1).astype(jnp.int32) - 1
    )
    slot_place = choices_flat * CAP + slot_index
    pick_table = (
        slot_place[:, None] == jnp.arange(E * CAP, dtype=jnp.int32)[None, :]
    ).astype(jnp.bfloat16).reshape(token_count, top_count, E * CAP)
    occupancy = jnp.sum(pick_table, axis=1).reshape(token_count, E, 1, CAP)
    send_table = jnp.broadcast_to(occupancy, (token_count, E, 2, CAP)).reshape(token_count, -1)
    device_count = lax.axis_size(("row", "col", "rep"))
    per_device = expert_gate_up.shape[0]
    outgoing = (
        jnp.einsum("tj,td->jd", send_table, normed_post, preferred_element_type=jnp.float32)
        .astype(jnp.bfloat16)
        .reshape(device_count, per_device, CAP, model_width)
    )
    produced = expert_apply(
        lax.all_to_all(outgoing, ("row", "col", "rep"), split_axis=0, concat_axis=0, tiled=True),
        expert_gate_up,
        expert_down,
    )
    returned = lax.all_to_all(
        produced, ("row", "col", "rep"), split_axis=0, concat_axis=0, tiled=True
    )
    returned = returned.reshape(E, 2, CAP, model_width)
    picked_first = jnp.einsum(
        "tkp,pd->tkd",
        pick_table,
        returned[:, 0].reshape(E * CAP, model_width),
        preferred_element_type=jnp.float32,
    )
    picked_second = jnp.einsum(
        "tkp,pd->tkd",
        pick_table,
        returned[:, 1].reshape(E * CAP, model_width),
        preferred_element_type=jnp.float32,
    )
    picked = picked_first + picked_second
    mixture = jnp.sum(picked * gate_weights[0][:, :, None], axis=1)
    layer_out = (residual.astype(jnp.float32) + mixture).astype(jnp.bfloat16)
    return (attention.astype(jnp.bfloat16)[None], layer_out[None])


def solution(mesh):
    in_specs = (
        P("rep", ("row", "col"), None),
        P("rep", None),
        P(("row", "col", "rep"), None),
        P(),
        P(),
        P(),
        P(),
        P(),
        P(),
        P(),
        P(),
        P("rep", ("row", "col"), None),
        P("rep", ("row", "col"), None),
        P(("row", "col", "rep"), None, None),
        P(("row", "col", "rep"), None, None),
    )
    out_specs = (P("rep", ("row", "col"), None), P("rep", ("row", "col"), None))
    return jax.shard_map(
        on_device, mesh=mesh, in_specs=in_specs, out_specs=out_specs, check_vma=False
    )
```

```python
import jax
import jax.numpy as jnp
from jax import lax
from jax.sharding import PartitionSpec as P

E = 64
CAP = 16


epsilon = 1e-06
rope_base = 50000.0
floor_value = -1e30


def rms_scale(values, gain_vector):
    mean_square = jnp.mean(values * values, axis=-1, keepdims=True)
    return values * lax.rsqrt(mean_square + epsilon) * gain_vector.astype(jnp.float32)


def rope_tables(positions, rope_width):
    halfway = rope_width // 2
    frequency = jnp.power(rope_base, -2.0 * jnp.arange(halfway, dtype=jnp.float32) / rope_width)
    angles = positions.astype(jnp.float32)[:, None] * frequency[None, :]
    return (jnp.cos(angles), jnp.sin(angles))


def rotate(values, cosine, sine_table):
    halfway = values.shape[-1] // 2
    leading = values[..., :halfway]
    trailing = values[..., halfway:]
    return jnp.concatenate(
        [leading * cosine - trailing * sine_table, trailing * cosine + leading * sine_table],
        axis=-1,
    )


def token_layout(group_lengths, first_place, row_count):
    ends = jnp.cumsum(group_lengths)
    starts = ends - group_lengths
    places = first_place + jnp.arange(row_count, dtype=jnp.int32)
    member = jnp.sum((places[:, None] >= ends[None, :]).astype(jnp.int32), axis=1)
    chosen = member[:, None] == jnp.arange(group_lengths.shape[0], dtype=jnp.int32)[None, :]
    offsets = jnp.sum(jnp.where(chosen, starts[None, :], 0), axis=1)
    return (member, places, places - offsets)


def make_queries(normed, positions, query_weight, latent_down, latent_gain, key_absorb):
    row_count = normed.shape[0]
    head_count = key_absorb.shape[0]
    plain_width = key_absorb.shape[1]
    latent_width = latent_gain.shape[0]
    projected = jnp.dot(normed, query_weight, preferred_element_type=jnp.float32).reshape(
        row_count, head_count, -1
    )
    rope_width = projected.shape[-1] - plain_width
    cosine, sine_table = rope_tables(positions, rope_width)
    query_plain = projected[..., :plain_width].astype(jnp.bfloat16)
    query_rotary = rotate(
        projected[..., plain_width:], cosine[:, None, :], sine_table[:, None, :]
    ).astype(jnp.bfloat16)
    query_latent = jnp.einsum(
        "thn,hnr->thr", query_plain, key_absorb, preferred_element_type=jnp.float32
    ).astype(jnp.bfloat16)
    query_rows = jnp.concatenate([query_latent, query_rotary], axis=-1)
    compressed = jnp.dot(normed, latent_down, preferred_element_type=jnp.float32)
    latent = rms_scale(compressed[:, :latent_width], latent_gain)
    key_rotary = rotate(compressed[:, latent_width:], cosine, sine_table)
    key_rows = jnp.concatenate([latent, key_rotary], axis=-1).astype(jnp.bfloat16)
    return (query_rows, key_rows)


def attend_block(state_now, query_rows, key_block, visible, scale_factor, latent_width):
    running_max, running_sum, weighted_sum = state_now
    scores = (
        lax.dot_general(
            query_rows, key_block, (((1,), (1,)), ((), ())), preferred_element_type=jnp.float32
        )
        * scale_factor
    )
    scores = jnp.where(visible, scores, -jnp.inf)
    new_max = jnp.maximum(running_max, jnp.max(scores, axis=1))
    rescale = jnp.exp(running_max - new_max)
    weights = jnp.exp(scores - new_max[:, None])
    running_sum = running_sum * rescale + jnp.sum(weights, axis=1)
    weighted_sum = weighted_sum * rescale[:, None] + jnp.dot(
        weights.astype(jnp.bfloat16),
        key_block[:, :latent_width],
        preferred_element_type=jnp.float32,
    )
    return (new_max, running_sum, weighted_sum)


def expert_apply(token_rows, expert_gate_up, expert_down):
    hidden_units = expert_down.shape[1]
    rows = token_rows.reshape(-1, token_rows.shape[-1])
    joint = jnp.dot(rows, expert_gate_up[0], preferred_element_type=jnp.float32)
    active = (jax.nn.silu(joint[:, :hidden_units]) * joint[:, hidden_units:]).astype(jnp.bfloat16)
    produced = jnp.dot(active, expert_down[0], preferred_element_type=jnp.float32)
    return produced.astype(jnp.bfloat16).reshape(token_rows.shape)


def gather_rows(rows, axes):
    count = lax.axis_size(axes)
    copies = jnp.broadcast_to(rows[None], (count,) + rows.shape)
    gathered = lax.all_to_all(copies, axes, split_axis=0, concat_axis=0, tiled=True)
    return gathered.reshape(count * rows.shape[0], rows.shape[1])


def on_device(
    hidden,
    lengths,
    prefix_latent,
    gain_in,
    query_weight,
    latent_down,
    latent_gain,
    key_absorb,
    value_up,
    output_weight,
    post_gain,
    routes,
    gate_weights,
    expert_gate_up,
    expert_down,
):
    token_count = hidden.shape[1]
    model_width = hidden.shape[2]
    head_count = key_absorb.shape[0]
    latent_width = latent_gain.shape[0]
    scale_factor = float(query_weight.shape[1] // head_count) ** (-0.5)
    group_lengths = lengths[0]
    prefix_total = prefix_latent.shape[0] * lax.axis_size(("row", "col", "rep"))
    first_place = lax.axis_index(("row", "col")) * token_count
    member, places, offsets = token_layout(group_lengths, first_place, token_count)
    own_tokens = hidden[0]
    normed = rms_scale(own_tokens.astype(jnp.float32), gain_in).astype(jnp.bfloat16)
    query_rows, key_rows = make_queries(
        normed, prefix_total + offsets, query_weight, latent_down, latent_gain, key_absorb
    )
    query_rows = query_rows.reshape(token_count * head_count, -1)
    row_member = jnp.repeat(member, head_count)
    row_places = jnp.repeat(places, head_count)
    row_total = token_count * head_count
    initial = (
        jnp.full((row_total,), floor_value, jnp.float32),
        jnp.zeros((row_total,), jnp.float32),
        jnp.zeros((row_total, latent_width), jnp.float32),
    )
    after_prefix = attend_block(
        initial,
        query_rows,
        gather_rows(prefix_latent, ("row", "col", "rep")),
        True,
        scale_factor,
        latent_width,
    )
    key_block = lax.all_gather(
        lax.all_gather(key_rows, "col", axis=0, tiled=True), "row", axis=0, tiled=True
    )
    block_member, block_places, block_offsets = token_layout(
        group_lengths, jnp.int32(0), key_block.shape[0]
    )
    visible = (row_member[:, None] == block_member[None, :]) & (
        row_places[:, None] >= block_places[None, :]
    )
    final_state = attend_block(
        after_prefix, query_rows, key_block, visible, scale_factor, latent_width
    )
    running_max, running_sum, weighted_sum = final_state
    mixed = (
        (weighted_sum / running_sum[:, None])
        .astype(jnp.bfloat16)
        .reshape(token_count, head_count, latent_width)
    )
    head_values = (
        jnp.einsum("thr,hrv->thv", mixed, value_up, preferred_element_type=jnp.float32)
        .astype(jnp.bfloat16)
        .reshape(token_count, -1)
    )
    attention = jnp.dot(head_values, output_weight, preferred_element_type=jnp.float32)
    residual = (own_tokens.astype(jnp.float32) + attention).astype(jnp.bfloat16)
    normed_post = rms_scale(residual.astype(jnp.float32), post_gain).astype(jnp.bfloat16)
    top_count = routes.shape[2]
    pair_count = token_count * top_count
    choices_flat = routes[0].reshape(-1)
    selected = (choices_flat[:, None] == jnp.arange(E, dtype=jnp.int32)[None, :]).astype(
        jnp.bfloat16
    )
    pair_ids = jnp.arange(pair_count, dtype=jnp.int32)
    lower = (pair_ids[:, None] >= pair_ids[None, :]).astype(jnp.bfloat16)
    running = jnp.dot(lower, selected, preferred_element_type=jnp.float32)
    slot_index = (
        jnp.sum(running * selected.astype(jnp.float32), axis=1).astype(jnp.int32) - 1
    )
    slot_place = choices_flat * CAP + slot_index
    pick_table = (
        slot_place[:, None] == jnp.arange(E * CAP, dtype=jnp.int32)[None, :]
    ).astype(jnp.bfloat16).reshape(token_count, top_count, E * CAP)
    occupancy = jnp.sum(pick_table, axis=1).reshape(token_count, E, 1, CAP)
    send_table = jnp.broadcast_to(occupancy, (token_count, E, 2, CAP))
    pick_slots = pick_table.reshape(token_count, top_count, E, CAP)
    device_count = lax.axis_size(("row", "col", "rep"))
    per_device = expert_gate_up.shape[0]
    chunk_count = 2
    chunk = CAP // chunk_count
    picked = None
    for part in range(chunk_count):
        window = slice(part * chunk, (part + 1) * chunk)
        outgoing = (
            jnp.einsum(
                "tj,td->jd",
                send_table[..., window].reshape(token_count, -1),
                normed_post,
                preferred_element_type=jnp.float32,
            )
            .astype(jnp.bfloat16)
            .reshape(device_count, per_device, chunk, model_width)
        )
        produced = expert_apply(
            lax.all_to_all(
                outgoing, ("row", "col", "rep"), split_axis=0, concat_axis=0, tiled=True
            ),
            expert_gate_up,
            expert_down,
        )
        returned = lax.all_to_all(
            produced, ("row", "col", "rep"), split_axis=0, concat_axis=0, tiled=True
        ).reshape(E, 2, chunk, model_width)
        table = pick_slots[..., window].reshape(token_count, top_count, E * chunk)
        for half in range(2):
            term = jnp.einsum(
                "tkp,pd->tkd",
                table,
                returned[:, half].reshape(E * chunk, model_width),
                preferred_element_type=jnp.float32,
            )
            picked = term if picked is None else picked + term
    mixture = jnp.sum(picked * gate_weights[0][:, :, None], axis=1)
    layer_out = (residual.astype(jnp.float32) + mixture).astype(jnp.bfloat16)
    return (attention.astype(jnp.bfloat16)[None], layer_out[None])


def solution(mesh):
    in_specs = (
        P("rep", ("row", "col"), None),
        P("rep", None),
        P(("row", "col", "rep"), None),
        P(),
        P(),
        P(),
        P(),
        P(),
        P(),
        P(),
        P(),
        P("rep", ("row", "col"), None),
        P("rep", ("row", "col"), None),
        P(("row", "col", "rep"), None, None),
        P(("row", "col", "rep"), None, None),
    )
    out_specs = (P("rep", ("row", "col"), None), P("rep", ("row", "col"), None))
    return jax.shard_map(
        on_device, mesh=mesh, in_specs=in_specs, out_specs=out_specs, check_vma=False
    )
```

```python
import jax
import jax.numpy as jnp
from jax import lax
from jax.sharding import PartitionSpec as P

E = 64
CAP = 16


epsilon = 1e-06
rope_base = 50000.0
floor_value = -1e30


def rms_scale(values, gain_vector):
    mean_square = jnp.mean(values * values, axis=-1, keepdims=True)
    return values * lax.rsqrt(mean_square + epsilon) * gain_vector.astype(jnp.float32)


def rope_tables(positions, rope_width):
    halfway = rope_width // 2
    frequency = jnp.power(rope_base, -2.0 * jnp.arange(halfway, dtype=jnp.float32) / rope_width)
    angles = positions.astype(jnp.float32)[:, None] * frequency[None, :]
    return (jnp.cos(angles), jnp.sin(angles))


def rotate(values, cosine, sine_table):
    halfway = values.shape[-1] // 2
    leading = values[..., :halfway]
    trailing = values[..., halfway:]
    return jnp.concatenate(
        [leading * cosine - trailing * sine_table, trailing * cosine + leading * sine_table],
        axis=-1,
    )


def token_layout(group_lengths, first_place, row_count):
    ends = jnp.cumsum(group_lengths)
    starts = ends - group_lengths
    places = first_place + jnp.arange(row_count, dtype=jnp.int32)
    member = jnp.sum((places[:, None] >= ends[None, :]).astype(jnp.int32), axis=1)
    chosen = member[:, None] == jnp.arange(group_lengths.shape[0], dtype=jnp.int32)[None, :]
    offsets = jnp.sum(jnp.where(chosen, starts[None, :], 0), axis=1)
    return (member, places, places - offsets)


def make_queries(normed, positions, query_weight, latent_down, latent_gain, key_absorb):
    row_count = normed.shape[0]
    head_count = key_absorb.shape[0]
    plain_width = key_absorb.shape[1]
    latent_width = latent_gain.shape[0]
    projected = jnp.dot(normed, query_weight, preferred_element_type=jnp.float32).reshape(
        row_count, head_count, -1
    )
    rope_width = projected.shape[-1] - plain_width
    cosine, sine_table = rope_tables(positions, rope_width)
    query_plain = projected[..., :plain_width].astype(jnp.bfloat16)
    query_rotary = rotate(
        projected[..., plain_width:], cosine[:, None, :], sine_table[:, None, :]
    ).astype(jnp.bfloat16)
    query_latent = jnp.einsum(
        "thn,hnr->thr", query_plain, key_absorb, preferred_element_type=jnp.float32
    ).astype(jnp.bfloat16)
    query_rows = jnp.concatenate([query_latent, query_rotary], axis=-1)
    compressed = jnp.dot(normed, latent_down, preferred_element_type=jnp.float32)
    latent = rms_scale(compressed[:, :latent_width], latent_gain)
    key_rotary = rotate(compressed[:, latent_width:], cosine, sine_table)
    key_rows = jnp.concatenate([latent, key_rotary], axis=-1).astype(jnp.bfloat16)
    return (query_rows, key_rows)


def attend_block(state_now, query_rows, key_block, visible, scale_factor, latent_width):
    running_max, running_sum, weighted_sum = state_now
    scores = (
        lax.dot_general(
            query_rows, key_block, (((1,), (1,)), ((), ())), preferred_element_type=jnp.float32
        )
        * scale_factor
    )
    scores = jnp.where(visible, scores, -jnp.inf)
    new_max = jnp.maximum(running_max, jnp.max(scores, axis=1))
    rescale = jnp.exp(running_max - new_max)
    weights = jnp.exp(scores - new_max[:, None])
    running_sum = running_sum * rescale + jnp.sum(weights, axis=1)
    weighted_sum = weighted_sum * rescale[:, None] + jnp.dot(
        weights.astype(jnp.bfloat16),
        key_block[:, :latent_width],
        preferred_element_type=jnp.float32,
    )
    return (new_max, running_sum, weighted_sum)


def expert_apply(token_rows, expert_gate_up, expert_down):
    hidden_units = expert_down.shape[1]
    rows = token_rows.reshape(-1, token_rows.shape[-1])
    joint = jnp.dot(rows, expert_gate_up[0], preferred_element_type=jnp.float32)
    active = (jax.nn.silu(joint[:, :hidden_units]) * joint[:, hidden_units:]).astype(jnp.bfloat16)
    produced = jnp.dot(active, expert_down[0], preferred_element_type=jnp.float32)
    return produced.astype(jnp.bfloat16).reshape(token_rows.shape)


def gather_rows(rows, axes):
    count = lax.axis_size(axes)
    copies = jnp.broadcast_to(rows[None], (count,) + rows.shape)
    gathered = lax.all_to_all(copies, axes, split_axis=0, concat_axis=0, tiled=True)
    return gathered.reshape(count * rows.shape[0], rows.shape[1])


def on_device(
    hidden,
    lengths,
    prefix_latent,
    gain_in,
    query_weight,
    latent_down,
    latent_gain,
    key_absorb,
    value_up,
    output_weight,
    post_gain,
    routes,
    gate_weights,
    expert_gate_up,
    expert_down,
):
    token_count = hidden.shape[1]
    model_width = hidden.shape[2]
    head_count = key_absorb.shape[0]
    latent_width = latent_gain.shape[0]
    scale_factor = float(query_weight.shape[1] // head_count) ** (-0.5)
    group_lengths = lengths[0]
    prefix_total = prefix_latent.shape[0] * lax.axis_size(("row", "col", "rep"))
    first_place = lax.axis_index(("row", "col")) * token_count
    member, places, offsets = token_layout(group_lengths, first_place, token_count)
    own_tokens = hidden[0]
    normed = rms_scale(own_tokens.astype(jnp.float32), gain_in).astype(jnp.bfloat16)
    query_rows, key_rows = make_queries(
        normed, prefix_total + offsets, query_weight, latent_down, latent_gain, key_absorb
    )
    query_rows = query_rows.reshape(token_count * head_count, -1)
    row_member = jnp.repeat(member, head_count)
    row_places = jnp.repeat(places, head_count)
    row_total = token_count * head_count
    initial = (
        jnp.full((row_total,), floor_value, jnp.float32),
        jnp.zeros((row_total,), jnp.float32),
        jnp.zeros((row_total, latent_width), jnp.float32),
    )
    after_prefix = attend_block(
        initial,
        query_rows,
        gather_rows(prefix_latent, ("row", "col", "rep")),
        True,
        scale_factor,
        latent_width,
    )
    key_block = lax.all_gather(
        lax.all_gather(key_rows, "col", axis=0, tiled=True), "row", axis=0, tiled=True
    )
    block_member, block_places, block_offsets = token_layout(
        group_lengths, jnp.int32(0), key_block.shape[0]
    )
    visible = (row_member[:, None] == block_member[None, :]) & (
        row_places[:, None] >= block_places[None, :]
    )
    final_state = attend_block(
        after_prefix, query_rows, key_block, visible, scale_factor, latent_width
    )
    running_max, running_sum, weighted_sum = final_state
    mixed = (
        (weighted_sum / running_sum[:, None])
        .astype(jnp.bfloat16)
        .reshape(token_count, head_count, latent_width)
    )
    head_values = (
        jnp.einsum("thr,hrv->thv", mixed, value_up, preferred_element_type=jnp.float32)
        .astype(jnp.bfloat16)
        .reshape(token_count, -1)
    )
    attention = jnp.dot(head_values, output_weight, preferred_element_type=jnp.float32)
    residual = (own_tokens.astype(jnp.float32) + attention).astype(jnp.bfloat16)
    normed_post = rms_scale(residual.astype(jnp.float32), post_gain).astype(jnp.bfloat16)
    top_count = routes.shape[2]
    pair_count = token_count * top_count
    choices_flat = routes[0].reshape(-1)
    selected = (choices_flat[:, None] == jnp.arange(E, dtype=jnp.int32)[None, :]).astype(
        jnp.bfloat16
    )
    pair_ids = jnp.arange(pair_count, dtype=jnp.int32)
    lower = (pair_ids[:, None] >= pair_ids[None, :]).astype(jnp.bfloat16)
    running = jnp.dot(lower, selected, preferred_element_type=jnp.float32)
    slot_index = (
        jnp.sum(running * selected.astype(jnp.float32), axis=1).astype(jnp.int32) - 1
    )
    slot_place = choices_flat * CAP + slot_index
    pick_table = (
        slot_place[:, None] == jnp.arange(E * CAP, dtype=jnp.int32)[None, :]
    ).astype(jnp.bfloat16).reshape(token_count, top_count, E * CAP)
    occupancy = jnp.sum(pick_table, axis=1).reshape(token_count, E, 1, CAP)
    send_table = jnp.broadcast_to(occupancy, (token_count, E, 2, CAP))
    pick_slots = pick_table.reshape(token_count, top_count, E, CAP)
    device_count = lax.axis_size(("row", "col", "rep"))
    per_device = expert_gate_up.shape[0]
    chunk_count = 2
    chunk = CAP // chunk_count
    gate_table = jnp.sum(
        pick_slots.astype(jnp.float32) * gate_weights[0][:, :, None, None], axis=1
    )
    mixture = None
    for part in range(chunk_count):
        window = slice(part * chunk, (part + 1) * chunk)
        outgoing = (
            jnp.einsum(
                "tj,td->jd",
                send_table[..., window].reshape(token_count, -1),
                normed_post,
                preferred_element_type=jnp.float32,
            )
            .astype(jnp.bfloat16)
            .reshape(device_count, per_device, chunk, model_width)
        )
        produced = expert_apply(
            lax.all_to_all(
                outgoing, ("row", "col", "rep"), split_axis=0, concat_axis=0, tiled=True
            ),
            expert_gate_up,
            expert_down,
        )
        returned = lax.all_to_all(
            produced, ("row", "col", "rep"), split_axis=0, concat_axis=0, tiled=True
        ).reshape(E, 2, chunk, model_width)
        paired = returned[:, 0].astype(jnp.float32) + returned[:, 1].astype(jnp.float32)
        term = jnp.dot(
            gate_table[..., window].reshape(token_count, E * chunk),
            paired.reshape(E * chunk, model_width),
            precision=lax.Precision.HIGHEST,
            preferred_element_type=jnp.float32,
        )
        mixture = term if mixture is None else mixture + term
    layer_out = (residual.astype(jnp.float32) + mixture).astype(jnp.bfloat16)
    return (attention.astype(jnp.bfloat16)[None], layer_out[None])


def solution(mesh):
    in_specs = (
        P("rep", ("row", "col"), None),
        P("rep", None),
        P(("row", "col", "rep"), None),
        P(),
        P(),
        P(),
        P(),
        P(),
        P(),
        P(),
        P(),
        P("rep", ("row", "col"), None),
        P("rep", ("row", "col"), None),
        P(("row", "col", "rep"), None, None),
        P(("row", "col", "rep"), None, None),
    )
    out_specs = (P("rep", ("row", "col"), None), P("rep", ("row", "col"), None))
    return jax.shard_map(
        on_device, mesh=mesh, in_specs=in_specs, out_specs=out_specs, check_vma=False
    )
```

```python
import jax
import jax.numpy as jnp
from jax import lax
from jax.sharding import PartitionSpec as P

E = 64
CAP = 16


epsilon = 1e-06
rope_base = 50000.0
floor_value = -1e30


def rms_scale(values, gain_vector):
    mean_square = jnp.mean(values * values, axis=-1, keepdims=True)
    return values * lax.rsqrt(mean_square + epsilon) * gain_vector.astype(jnp.float32)


def rope_tables(positions, rope_width):
    halfway = rope_width // 2
    frequency = jnp.power(rope_base, -2.0 * jnp.arange(halfway, dtype=jnp.float32) / rope_width)
    angles = positions.astype(jnp.float32)[:, None] * frequency[None, :]
    return (jnp.cos(angles), jnp.sin(angles))


def rotate(values, cosine, sine_table):
    halfway = values.shape[-1] // 2
    leading = values[..., :halfway]
    trailing = values[..., halfway:]
    return jnp.concatenate(
        [leading * cosine - trailing * sine_table, trailing * cosine + leading * sine_table],
        axis=-1,
    )


def token_layout(group_lengths, first_place, row_count):
    ends = jnp.cumsum(group_lengths)
    starts = ends - group_lengths
    places = first_place + jnp.arange(row_count, dtype=jnp.int32)
    member = jnp.sum((places[:, None] >= ends[None, :]).astype(jnp.int32), axis=1)
    chosen = member[:, None] == jnp.arange(group_lengths.shape[0], dtype=jnp.int32)[None, :]
    offsets = jnp.sum(jnp.where(chosen, starts[None, :], 0), axis=1)
    return (member, places, places - offsets)


def make_queries(normed, positions, query_weight, latent_down, latent_gain, key_absorb):
    row_count = normed.shape[0]
    head_count = key_absorb.shape[0]
    plain_width = key_absorb.shape[1]
    latent_width = latent_gain.shape[0]
    projected = lax.optimization_barrier(
        jnp.dot(normed, query_weight, preferred_element_type=jnp.float32)
    ).reshape(row_count, head_count, -1)
    rope_width = projected.shape[-1] - plain_width
    cosine, sine_table = rope_tables(positions, rope_width)
    query_plain = projected[..., :plain_width].astype(jnp.bfloat16)
    query_rotary = rotate(
        projected[..., plain_width:], cosine[:, None, :], sine_table[:, None, :]
    ).astype(jnp.bfloat16)
    query_latent = jnp.einsum(
        "thn,hnr->thr", query_plain, key_absorb, preferred_element_type=jnp.float32
    ).astype(jnp.bfloat16)
    query_rows = jnp.concatenate([query_latent, query_rotary], axis=-1)
    compressed = jnp.dot(normed, latent_down, preferred_element_type=jnp.float32)
    latent = rms_scale(compressed[:, :latent_width], latent_gain)
    key_rotary = rotate(compressed[:, latent_width:], cosine, sine_table)
    key_rows = jnp.concatenate([latent, key_rotary], axis=-1).astype(jnp.bfloat16)
    return (query_rows, key_rows)


def attend_block(state_now, query_rows, key_block, visible, scale_factor, latent_width):
    running_max, running_sum, weighted_sum = state_now
    scores = (
        lax.dot_general(
            query_rows, key_block, (((1,), (1,)), ((), ())), preferred_element_type=jnp.float32
        )
        * scale_factor
    )
    scores = jnp.where(visible, scores, -jnp.inf)
    new_max = jnp.maximum(running_max, jnp.max(scores, axis=1))
    rescale = jnp.exp(running_max - new_max)
    weights = jnp.exp(scores - new_max[:, None])
    running_sum = running_sum * rescale + jnp.sum(weights, axis=1)
    weighted_sum = weighted_sum * rescale[:, None] + jnp.dot(
        weights.astype(jnp.bfloat16),
        key_block[:, :latent_width],
        preferred_element_type=jnp.float32,
    )
    return (new_max, running_sum, weighted_sum)


def expert_apply(token_rows, expert_gate_up, expert_down):
    hidden_units = expert_down.shape[1]
    rows = token_rows.reshape(-1, token_rows.shape[-1])
    joint = jnp.dot(rows, expert_gate_up[0], preferred_element_type=jnp.float32)
    active = (jax.nn.silu(joint[:, :hidden_units]) * joint[:, hidden_units:]).astype(jnp.bfloat16)
    produced = jnp.dot(active, expert_down[0], preferred_element_type=jnp.float32)
    return produced.astype(jnp.bfloat16).reshape(token_rows.shape)


def gather_rows(rows, axes):
    count = lax.axis_size(axes)
    copies = jnp.broadcast_to(rows[None], (count,) + rows.shape)
    gathered = lax.all_to_all(copies, axes, split_axis=0, concat_axis=0, tiled=True)
    return gathered.reshape(count * rows.shape[0], rows.shape[1])


def on_device(
    hidden,
    lengths,
    prefix_latent,
    gain_in,
    query_weight,
    latent_down,
    latent_gain,
    key_absorb,
    value_up,
    output_weight,
    post_gain,
    routes,
    gate_weights,
    expert_gate_up,
    expert_down,
):
    token_count = hidden.shape[1]
    model_width = hidden.shape[2]
    head_count = key_absorb.shape[0]
    latent_width = latent_gain.shape[0]
    scale_factor = float(query_weight.shape[1] // head_count) ** (-0.5)
    group_lengths = lengths[0]
    prefix_total = prefix_latent.shape[0] * lax.axis_size(("row", "col", "rep"))
    first_place = lax.axis_index(("row", "col")) * token_count
    member, places, offsets = token_layout(group_lengths, first_place, token_count)
    own_tokens = hidden[0]
    normed = rms_scale(own_tokens.astype(jnp.float32), gain_in).astype(jnp.bfloat16)
    query_rows, key_rows = make_queries(
        normed, prefix_total + offsets, query_weight, latent_down, latent_gain, key_absorb
    )
    query_rows = query_rows.reshape(token_count * head_count, -1)
    row_member = jnp.repeat(member, head_count)
    row_places = jnp.repeat(places, head_count)
    row_total = token_count * head_count
    initial = (
        jnp.full((row_total,), floor_value, jnp.float32),
        jnp.zeros((row_total,), jnp.float32),
        jnp.zeros((row_total, latent_width), jnp.float32),
    )
    after_prefix = attend_block(
        initial,
        query_rows,
        gather_rows(prefix_latent, ("row", "col", "rep")),
        True,
        scale_factor,
        latent_width,
    )
    key_block = lax.all_gather(
        lax.all_gather(key_rows, "col", axis=0, tiled=True), "row", axis=0, tiled=True
    )
    block_member, block_places, block_offsets = token_layout(
        group_lengths, jnp.int32(0), key_block.shape[0]
    )
    visible = (row_member[:, None] == block_member[None, :]) & (
        row_places[:, None] >= block_places[None, :]
    )
    final_state = attend_block(
        after_prefix, query_rows, key_block, visible, scale_factor, latent_width
    )
    running_max, running_sum, weighted_sum = final_state
    mixed = (
        (weighted_sum / running_sum[:, None])
        .astype(jnp.bfloat16)
        .reshape(token_count, head_count, latent_width)
    )
    head_values = (
        jnp.einsum("thr,hrv->thv", mixed, value_up, preferred_element_type=jnp.float32)
        .astype(jnp.bfloat16)
        .reshape(token_count, -1)
    )
    attention = jnp.dot(head_values, output_weight, preferred_element_type=jnp.float32)
    residual = (own_tokens.astype(jnp.float32) + attention).astype(jnp.bfloat16)
    normed_post = rms_scale(residual.astype(jnp.float32), post_gain).astype(jnp.bfloat16)
    top_count = routes.shape[2]
    pair_count = token_count * top_count
    choices_flat = routes[0].reshape(-1)
    selected = (choices_flat[:, None] == jnp.arange(E, dtype=jnp.int32)[None, :]).astype(
        jnp.bfloat16
    )
    pair_ids = jnp.arange(pair_count, dtype=jnp.int32)
    lower = (pair_ids[:, None] >= pair_ids[None, :]).astype(jnp.bfloat16)
    running = jnp.dot(lower, selected, preferred_element_type=jnp.float32)
    slot_index = (
        jnp.sum(running * selected.astype(jnp.float32), axis=1).astype(jnp.int32) - 1
    )
    slot_place = choices_flat * CAP + slot_index
    pick_table = (
        slot_place[:, None] == jnp.arange(E * CAP, dtype=jnp.int32)[None, :]
    ).astype(jnp.bfloat16).reshape(token_count, top_count, E * CAP)
    occupancy = jnp.sum(pick_table, axis=1).reshape(token_count, E, 1, CAP)
    send_table = jnp.broadcast_to(occupancy, (token_count, E, 2, CAP))
    pick_slots = pick_table.reshape(token_count, top_count, E, CAP)
    device_count = lax.axis_size(("row", "col", "rep"))
    per_device = expert_gate_up.shape[0]
    chunk_count = 2
    chunk = CAP // chunk_count
    gate_table = jnp.sum(
        pick_slots.astype(jnp.float32) * gate_weights[0][:, :, None, None], axis=1
    )
    mixture = None
    for part in range(chunk_count):
        window = slice(part * chunk, (part + 1) * chunk)
        outgoing = (
            jnp.einsum(
                "tj,td->jd",
                send_table[..., window].reshape(token_count, -1),
                normed_post,
                preferred_element_type=jnp.float32,
            )
            .astype(jnp.bfloat16)
            .reshape(device_count, per_device, chunk, model_width)
        )
        produced = expert_apply(
            lax.all_to_all(
                outgoing, ("row", "col", "rep"), split_axis=0, concat_axis=0, tiled=True
            ),
            expert_gate_up,
            expert_down,
        )
        returned = lax.all_to_all(
            produced, ("row", "col", "rep"), split_axis=0, concat_axis=0, tiled=True
        ).reshape(E, 2, chunk, model_width)
        paired = returned[:, 0].astype(jnp.float32) + returned[:, 1].astype(jnp.float32)
        term = jnp.dot(
            gate_table[..., window].reshape(token_count, E * chunk),
            paired.reshape(E * chunk, model_width),
            precision=lax.Precision.HIGHEST,
            preferred_element_type=jnp.float32,
        )
        mixture = term if mixture is None else mixture + term
    layer_out = (residual.astype(jnp.float32) + mixture).astype(jnp.bfloat16)
    return (attention.astype(jnp.bfloat16)[None], layer_out[None])


def solution(mesh):
    in_specs = (
        P("rep", ("row", "col"), None),
        P("rep", None),
        P(("row", "col", "rep"), None),
        P(),
        P(),
        P(),
        P(),
        P(),
        P(),
        P(),
        P(),
        P("rep", ("row", "col"), None),
        P("rep", ("row", "col"), None),
        P(("row", "col", "rep"), None, None),
        P(("row", "col", "rep"), None, None),
    )
    out_specs = (P("rep", ("row", "col"), None), P("rep", ("row", "col"), None))
    return jax.shard_map(
        on_device, mesh=mesh, in_specs=in_specs, out_specs=out_specs, check_vma=False
    )
```

```python
import jax
import jax.numpy as jnp
from jax import lax
from jax.sharding import PartitionSpec as P

E = 64
CAP = 16


epsilon = 1e-06
rope_base = 50000.0
floor_value = -1e30


def rms_scale(values, gain_vector):
    mean_square = jnp.mean(values * values, axis=-1, keepdims=True)
    return values * lax.rsqrt(mean_square + epsilon) * gain_vector.astype(jnp.float32)


def rope_tables(positions, rope_width):
    halfway = rope_width // 2
    frequency = jnp.power(rope_base, -2.0 * jnp.arange(halfway, dtype=jnp.float32) / rope_width)
    angles = positions.astype(jnp.float32)[:, None] * frequency[None, :]
    return (jnp.cos(angles), jnp.sin(angles))


def rotate(values, cosine, sine_table):
    halfway = values.shape[-1] // 2
    leading = values[..., :halfway]
    trailing = values[..., halfway:]
    return jnp.concatenate(
        [leading * cosine - trailing * sine_table, trailing * cosine + leading * sine_table],
        axis=-1,
    )


def token_layout(group_lengths, first_place, row_count):
    ends = jnp.cumsum(group_lengths)
    starts = ends - group_lengths
    places = first_place + jnp.arange(row_count, dtype=jnp.int32)
    member = jnp.sum((places[:, None] >= ends[None, :]).astype(jnp.int32), axis=1)
    chosen = member[:, None] == jnp.arange(group_lengths.shape[0], dtype=jnp.int32)[None, :]
    offsets = jnp.sum(jnp.where(chosen, starts[None, :], 0), axis=1)
    return (member, places, places - offsets)


def make_queries(normed, positions, query_weight, latent_down, latent_gain, key_absorb):
    row_count = normed.shape[0]
    head_count = key_absorb.shape[0]
    plain_width = key_absorb.shape[1]
    latent_width = latent_gain.shape[0]
    projected = lax.optimization_barrier(
        jnp.dot(normed, query_weight, preferred_element_type=jnp.float32)
    ).reshape(row_count, head_count, -1)
    rope_width = projected.shape[-1] - plain_width
    cosine, sine_table = rope_tables(positions, rope_width)
    query_plain = projected[..., :plain_width].astype(jnp.bfloat16)
    query_rotary = rotate(
        projected[..., plain_width:], cosine[:, None, :], sine_table[:, None, :]
    ).astype(jnp.bfloat16)
    query_latent = jnp.einsum(
        "thn,hnr->thr", query_plain, key_absorb, preferred_element_type=jnp.float32
    ).astype(jnp.bfloat16)
    query_rows = jnp.concatenate([query_latent, query_rotary], axis=-1)
    compressed = jnp.dot(normed, latent_down, preferred_element_type=jnp.float32)
    latent = rms_scale(compressed[:, :latent_width], latent_gain)
    key_rotary = rotate(compressed[:, latent_width:], cosine, sine_table)
    key_rows = jnp.concatenate([latent, key_rotary], axis=-1).astype(jnp.bfloat16)
    return (query_rows, key_rows)


def attend_block(state_now, query_rows, key_block, visible, scale_factor, latent_width):
    running_max, running_sum, weighted_sum = state_now
    scores = (
        lax.dot_general(
            query_rows, key_block, (((1,), (1,)), ((), ())), preferred_element_type=jnp.float32
        )
        * scale_factor
    )
    scores = jnp.where(visible, scores, -jnp.inf)
    new_max = jnp.maximum(running_max, jnp.max(scores, axis=1))
    rescale = jnp.exp(running_max - new_max)
    weights = jnp.exp(scores - new_max[:, None])
    running_sum = running_sum * rescale + jnp.sum(weights, axis=1)
    weighted_sum = weighted_sum * rescale[:, None] + jnp.dot(
        weights.astype(jnp.bfloat16),
        key_block[:, :latent_width],
        preferred_element_type=jnp.float32,
    )
    return (new_max, running_sum, weighted_sum)


def expert_apply(token_rows, expert_gate_up, expert_down):
    hidden_units = expert_down.shape[1]
    rows = token_rows.reshape(-1, token_rows.shape[-1])
    joint = jnp.dot(rows, expert_gate_up[0], preferred_element_type=jnp.float32)
    active = (jax.nn.silu(joint[:, :hidden_units]) * joint[:, hidden_units:]).astype(jnp.bfloat16)
    produced = jnp.dot(active, expert_down[0], preferred_element_type=jnp.float32)
    return produced.astype(jnp.bfloat16).reshape(token_rows.shape)


def gather_rows(rows, axes):
    count = lax.axis_size(axes)
    copies = jnp.broadcast_to(rows[None], (count,) + rows.shape)
    gathered = lax.all_to_all(copies, axes, split_axis=0, concat_axis=0, tiled=True)
    return gathered.reshape(count * rows.shape[0], rows.shape[1])


def on_device(
    hidden,
    lengths,
    prefix_latent,
    gain_in,
    query_weight,
    latent_down,
    latent_gain,
    key_absorb,
    value_up,
    output_weight,
    post_gain,
    routes,
    gate_weights,
    expert_gate_up,
    expert_down,
):
    token_count = hidden.shape[1]
    model_width = hidden.shape[2]
    head_count = key_absorb.shape[0]
    latent_width = latent_gain.shape[0]
    scale_factor = float(query_weight.shape[1] // head_count) ** (-0.5)
    group_lengths = lengths[0]
    prefix_total = prefix_latent.shape[0] * lax.axis_size(("row", "col", "rep"))
    first_place = lax.axis_index(("row", "col")) * token_count
    member, places, offsets = token_layout(group_lengths, first_place, token_count)
    own_tokens = hidden[0]
    normed = rms_scale(own_tokens.astype(jnp.float32), gain_in).astype(jnp.bfloat16)
    query_rows, key_rows = make_queries(
        normed, prefix_total + offsets, query_weight, latent_down, latent_gain, key_absorb
    )
    query_rows = query_rows.reshape(token_count * head_count, -1)
    row_member = jnp.repeat(member, head_count)
    row_places = jnp.repeat(places, head_count)
    row_total = token_count * head_count
    initial = (
        jnp.full((row_total,), floor_value, jnp.float32),
        jnp.zeros((row_total,), jnp.float32),
        jnp.zeros((row_total, latent_width), jnp.float32),
    )
    prefix_rows = gather_rows(prefix_latent, ("row", "col", "rep"))
    after_prefix = attend_block(
        initial,
        query_rows,
        prefix_rows,
        True,
        scale_factor,
        latent_width,
    )
    key_block = lax.all_gather(key_rows, ("row", "col"), axis=0, tiled=True)
    block_member, block_places, _ = token_layout(group_lengths, jnp.int32(0), key_block.shape[0])
    visible = (row_member[:, None] == block_member[None, :]) & (
        row_places[:, None] >= block_places[None, :]
    )
    final_state = attend_block(
        after_prefix, query_rows, key_block, visible, scale_factor, latent_width
    )
    _, running_sum, weighted_sum = final_state
    mixed = (
        (weighted_sum / running_sum[:, None])
        .astype(jnp.bfloat16)
        .reshape(token_count, head_count, latent_width)
    )
    head_values = (
        jnp.einsum("thr,hrv->thv", mixed, value_up, preferred_element_type=jnp.float32)
        .astype(jnp.bfloat16)
        .reshape(token_count, -1)
    )
    attention = jnp.dot(head_values, output_weight, preferred_element_type=jnp.float32)
    residual = (own_tokens.astype(jnp.float32) + attention).astype(jnp.bfloat16)
    normed_post = rms_scale(residual.astype(jnp.float32), post_gain).astype(jnp.bfloat16)
    top_count = routes.shape[2]
    pair_count = token_count * top_count
    choices_flat = routes[0].reshape(-1)
    selected = (choices_flat[:, None] == jnp.arange(E, dtype=jnp.int32)[None, :]).astype(
        jnp.bfloat16
    )
    pair_ids = jnp.arange(pair_count, dtype=jnp.int32)
    lower = (pair_ids[:, None] >= pair_ids[None, :]).astype(jnp.bfloat16)
    running = jnp.dot(lower, selected, preferred_element_type=jnp.float32)
    slot_index = (
        jnp.sum(running * selected.astype(jnp.float32), axis=1).astype(jnp.int32) - 1
    )
    slot_place = choices_flat * CAP + slot_index
    pick_table = (
        slot_place[:, None] == jnp.arange(E * CAP, dtype=jnp.int32)[None, :]
    ).astype(jnp.bfloat16).reshape(token_count, top_count, E * CAP)
    occupancy = jnp.sum(pick_table, axis=1).reshape(token_count, E, 1, CAP)
    send_table = jnp.broadcast_to(occupancy, (token_count, E, 2, CAP))
    pick_slots = pick_table.reshape(token_count, top_count, E, CAP)
    device_count = lax.axis_size(("row", "col", "rep"))
    per_device = expert_gate_up.shape[0]
    chunk_count = 2
    chunk = CAP // chunk_count
    gate_table = jnp.sum(
        pick_slots.astype(jnp.float32) * gate_weights[0][:, :, None, None], axis=1
    )
    mixture = None
    for part in range(chunk_count):
        window = slice(part * chunk, (part + 1) * chunk)
        outgoing = (
            jnp.einsum(
                "tj,td->jd",
                send_table[..., window].reshape(token_count, -1),
                normed_post,
                preferred_element_type=jnp.float32,
            )
            .astype(jnp.bfloat16)
            .reshape(device_count, per_device, chunk, model_width)
        )
        produced = expert_apply(
            lax.all_to_all(
                outgoing, ("row", "col", "rep"), split_axis=0, concat_axis=0, tiled=True
            ),
            expert_gate_up,
            expert_down,
        )
        returned = lax.all_to_all(
            produced, ("row", "col", "rep"), split_axis=0, concat_axis=0, tiled=True
        ).reshape(E, 2, chunk, model_width)
        paired = returned[:, 0].astype(jnp.float32) + returned[:, 1].astype(jnp.float32)
        term = jnp.dot(
            gate_table[..., window].reshape(token_count, E * chunk),
            paired.reshape(E * chunk, model_width),
            precision=lax.Precision.HIGHEST,
            preferred_element_type=jnp.float32,
        )
        mixture = term if mixture is None else mixture + term
    layer_out = (residual.astype(jnp.float32) + mixture).astype(jnp.bfloat16)
    return (attention.astype(jnp.bfloat16)[None], layer_out[None])


def solution(mesh):
    in_specs = (
        P("rep", ("row", "col"), None),
        P("rep", None),
        P(("row", "col", "rep"), None),
        P(),
        P(),
        P(),
        P(),
        P(),
        P(),
        P(),
        P(),
        P("rep", ("row", "col"), None),
        P("rep", ("row", "col"), None),
        P(("row", "col", "rep"), None, None),
        P(("row", "col", "rep"), None, None),
    )
    out_specs = (P("rep", ("row", "col"), None), P("rep", ("row", "col"), None))

    return jax.shard_map(on_device, mesh=mesh, in_specs=in_specs, out_specs=out_specs, check_vma=False)
```

```python
import jax
import jax.numpy as jnp
from jax import lax
from jax.sharding import PartitionSpec as P

E = 64
CAP = 16


epsilon = 1e-06
rope_base = 50000.0
floor_value = -1e30


def rms_scale(values, gain_vector):
    mean_square = jnp.mean(values * values, axis=-1, keepdims=True)
    return values * lax.rsqrt(mean_square + epsilon) * gain_vector.astype(jnp.float32)


def rope_tables(positions, rope_width):
    halfway = rope_width // 2
    frequency = jnp.power(rope_base, -2.0 * jnp.arange(halfway, dtype=jnp.float32) / rope_width)
    angles = positions.astype(jnp.float32)[:, None] * frequency[None, :]
    return (jnp.cos(angles), jnp.sin(angles))


def rotate(values, cosine, sine_table):
    halfway = values.shape[-1] // 2
    leading = values[..., :halfway]
    trailing = values[..., halfway:]
    return jnp.concatenate(
        [leading * cosine - trailing * sine_table, trailing * cosine + leading * sine_table],
        axis=-1,
    )


def token_layout(group_lengths, first_place, row_count):
    ends = jnp.cumsum(group_lengths)
    starts = ends - group_lengths
    places = first_place + jnp.arange(row_count, dtype=jnp.int32)
    member = jnp.sum((places[:, None] >= ends[None, :]).astype(jnp.int32), axis=1)
    chosen = member[:, None] == jnp.arange(group_lengths.shape[0], dtype=jnp.int32)[None, :]
    offsets = jnp.sum(jnp.where(chosen, starts[None, :], 0), axis=1)
    return (member, places, places - offsets)


def make_queries(normed, positions, query_weight, latent_down, latent_gain, key_absorb):
    row_count = normed.shape[0]
    head_count = key_absorb.shape[0]
    plain_width = key_absorb.shape[1]
    latent_width = latent_gain.shape[0]
    projected = lax.optimization_barrier(
        jnp.dot(normed, query_weight, preferred_element_type=jnp.float32)
    ).reshape(row_count, head_count, -1)
    rope_width = projected.shape[-1] - plain_width
    cosine, sine_table = rope_tables(positions, rope_width)
    query_plain = projected[..., :plain_width].astype(jnp.bfloat16)
    query_rotary = rotate(
        projected[..., plain_width:], cosine[:, None, :], sine_table[:, None, :]
    ).astype(jnp.bfloat16)
    query_latent = jnp.einsum(
        "thn,hnr->thr", query_plain, key_absorb, preferred_element_type=jnp.float32
    ).astype(jnp.bfloat16)
    query_rows = jnp.concatenate([query_latent, query_rotary], axis=-1)
    compressed = jnp.dot(normed, latent_down, preferred_element_type=jnp.float32)
    latent = rms_scale(compressed[:, :latent_width], latent_gain)
    key_rotary = rotate(compressed[:, latent_width:], cosine, sine_table)
    key_rows = jnp.concatenate([latent, key_rotary], axis=-1).astype(jnp.bfloat16)
    return (query_rows, key_rows)


def attend_block(state_now, query_rows, key_block, visible, scale_factor, latent_width):
    running_max, running_sum, weighted_sum = state_now
    scores = (
        lax.dot_general(
            query_rows, key_block, (((1,), (1,)), ((), ())), preferred_element_type=jnp.float32
        )
        * scale_factor
    )
    scores = jnp.where(visible, scores, -jnp.inf)
    new_max = jnp.maximum(running_max, jnp.max(scores, axis=1))
    rescale = jnp.exp(running_max - new_max)
    weights = jnp.exp(scores - new_max[:, None])
    running_sum = running_sum * rescale + jnp.sum(weights, axis=1)
    weighted_sum = weighted_sum * rescale[:, None] + jnp.dot(
        weights.astype(jnp.bfloat16),
        key_block[:, :latent_width],
        preferred_element_type=jnp.float32,
    )
    return (new_max, running_sum, weighted_sum)


def expert_apply(token_rows, expert_gate_up, expert_down):
    hidden_units = expert_down.shape[1]
    rows = token_rows.reshape(-1, token_rows.shape[-1])
    joint = jnp.dot(rows, expert_gate_up[0], preferred_element_type=jnp.float32)
    active = (jax.nn.silu(joint[:, :hidden_units]) * joint[:, hidden_units:]).astype(jnp.bfloat16)
    produced = jnp.dot(active, expert_down[0], preferred_element_type=jnp.float32)
    return produced.astype(jnp.bfloat16).reshape(token_rows.shape)


def gather_rows(rows, axes):
    count = lax.axis_size(axes)
    copies = jnp.broadcast_to(rows[None], (count,) + rows.shape)
    gathered = lax.all_to_all(copies, axes, split_axis=0, concat_axis=0, tiled=True)
    return gathered.reshape(count * rows.shape[0], rows.shape[1])


def on_device(
    hidden,
    lengths,
    prefix_latent,
    gain_in,
    query_weight,
    latent_down,
    latent_gain,
    key_absorb,
    value_up,
    output_weight,
    post_gain,
    routes,
    gate_weights,
    expert_gate_up,
    expert_down,
):
    token_count = hidden.shape[1]
    model_width = hidden.shape[2]
    head_count = key_absorb.shape[0]
    latent_width = latent_gain.shape[0]
    scale_factor = float(query_weight.shape[1] // head_count) ** (-0.5)
    group_lengths = lengths[0]
    prefix_total = prefix_latent.shape[0] * lax.axis_size(("row", "col", "rep"))
    first_place = lax.axis_index(("row", "col")) * token_count
    member, places, offsets = token_layout(group_lengths, first_place, token_count)
    own_tokens = hidden[0]
    normed = rms_scale(own_tokens.astype(jnp.float32), gain_in).astype(jnp.bfloat16)
    query_rows, key_rows = make_queries(
        normed, prefix_total + offsets, query_weight, latent_down, latent_gain, key_absorb
    )
    query_rows = query_rows.reshape(token_count * head_count, -1)
    row_member = jnp.repeat(member, head_count)
    row_places = jnp.repeat(places, head_count)
    row_total = token_count * head_count
    initial = (
        jnp.full((row_total,), floor_value, jnp.float32),
        jnp.zeros((row_total,), jnp.float32),
        jnp.zeros((row_total, latent_width), jnp.float32),
    )
    after_prefix = attend_block(
        initial,
        query_rows,
        gather_rows(prefix_latent, ("row", "col", "rep")),
        True,
        scale_factor,
        latent_width,
    )
    key_block = lax.all_gather(
        lax.all_gather(key_rows, "col", axis=0, tiled=True), "row", axis=0, tiled=True
    )
    block_member, block_places, block_offsets = token_layout(
        group_lengths, jnp.int32(0), key_block.shape[0]
    )
    visible = (row_member[:, None] == block_member[None, :]) & (
        row_places[:, None] >= block_places[None, :]
    )
    final_state = attend_block(
        after_prefix, query_rows, key_block, visible, scale_factor, latent_width
    )
    running_max, running_sum, weighted_sum = final_state
    mixed = (
        (weighted_sum / running_sum[:, None])
        .astype(jnp.bfloat16)
        .reshape(token_count, head_count, latent_width)
    )
    head_values = (
        jnp.einsum("thr,hrv->thv", mixed, value_up, preferred_element_type=jnp.float32)
        .astype(jnp.bfloat16)
        .reshape(token_count, -1)
    )
    attention = jnp.dot(head_values, output_weight, preferred_element_type=jnp.float32)
    residual = (own_tokens.astype(jnp.float32) + attention).astype(jnp.bfloat16)
    normed_post = rms_scale(residual.astype(jnp.float32), post_gain).astype(jnp.bfloat16)
    top_count = routes.shape[2]
    pair_count = token_count * top_count
    choices_flat = routes[0].reshape(-1)
    selected = (choices_flat[:, None] == jnp.arange(E, dtype=jnp.int32)[None, :]).astype(
        jnp.bfloat16
    )
    pair_ids = jnp.arange(pair_count, dtype=jnp.int32)
    lower = (pair_ids[:, None] >= pair_ids[None, :]).astype(jnp.bfloat16)
    running = jnp.dot(lower, selected, preferred_element_type=jnp.float32)
    slot_index = (
        jnp.sum(running * selected.astype(jnp.float32), axis=1).astype(jnp.int32) - 1
    )
    slot_place = choices_flat * CAP + slot_index
    pick_table = (
        slot_place[:, None] == jnp.arange(E * CAP, dtype=jnp.int32)[None, :]
    ).astype(jnp.bfloat16).reshape(token_count, top_count, E * CAP)
    occupancy = jnp.sum(pick_table, axis=1).reshape(token_count, E, 1, CAP)
    send_table = jnp.broadcast_to(occupancy, (token_count, E, 2, CAP))
    pick_slots = pick_table.reshape(token_count, top_count, E, CAP)
    device_count = lax.axis_size(("row", "col", "rep"))
    per_device = expert_gate_up.shape[0]
    chunk_count = 4
    chunk = CAP // chunk_count
    gate_table = jnp.sum(
        pick_slots.astype(jnp.float32) * gate_weights[0][:, :, None, None], axis=1
    )
    mixture = None
    for part in range(chunk_count):
        window = slice(part * chunk, (part + 1) * chunk)
        outgoing = (
            jnp.einsum(
                "tj,td->jd",
                send_table[..., window].reshape(token_count, -1),
                normed_post,
                preferred_element_type=jnp.float32,
            )
            .astype(jnp.bfloat16)
            .reshape(device_count, per_device, chunk, model_width)
        )
        produced = expert_apply(
            lax.all_to_all(
                outgoing, ("row", "col", "rep"), split_axis=0, concat_axis=0, tiled=True
            ),
            expert_gate_up,
            expert_down,
        )
        returned = lax.all_to_all(
            produced, ("row", "col", "rep"), split_axis=0, concat_axis=0, tiled=True
        ).reshape(E, 2, chunk, model_width)
        paired = returned[:, 0].astype(jnp.float32) + returned[:, 1].astype(jnp.float32)
        term = jnp.dot(
            gate_table[..., window].reshape(token_count, E * chunk),
            paired.reshape(E * chunk, model_width),
            precision=lax.Precision.HIGHEST,
            preferred_element_type=jnp.float32,
        )
        mixture = term if mixture is None else mixture + term
    layer_out = (residual.astype(jnp.float32) + mixture).astype(jnp.bfloat16)
    return (attention.astype(jnp.bfloat16)[None], layer_out[None])


def solution(mesh):
    in_specs = (
        P("rep", ("row", "col"), None),
        P("rep", None),
        P(("row", "col", "rep"), None),
        P(),
        P(),
        P(),
        P(),
        P(),
        P(),
        P(),
        P(),
        P("rep", ("row", "col"), None),
        P("rep", ("row", "col"), None),
        P(("row", "col", "rep"), None, None),
        P(("row", "col", "rep"), None, None),
    )
    out_specs = (P("rep", ("row", "col"), None), P("rep", ("row", "col"), None))
    return jax.shard_map(
        on_device, mesh=mesh, in_specs=in_specs, out_specs=out_specs, check_vma=False
    )
```

```python
import jax
import jax.numpy as jnp
from jax import lax
from jax.sharding import PartitionSpec as P

E = 64
CAP = 16


epsilon = 1e-06
rope_base = 50000.0
floor_value = -1e30


def rms_scale(values, gain_vector):
    mean_square = jnp.mean(values * values, axis=-1, keepdims=True)
    return values * lax.rsqrt(mean_square + epsilon) * gain_vector.astype(jnp.float32)


def rope_tables(positions, rope_width):
    halfway = rope_width // 2
    frequency = jnp.power(rope_base, -2.0 * jnp.arange(halfway, dtype=jnp.float32) / rope_width)
    angles = positions.astype(jnp.float32)[:, None] * frequency[None, :]
    return (jnp.cos(angles), jnp.sin(angles))


def rotate(values, cosine, sine_table):
    halfway = values.shape[-1] // 2
    leading = values[..., :halfway]
    trailing = values[..., halfway:]
    return jnp.concatenate(
        [leading * cosine - trailing * sine_table, trailing * cosine + leading * sine_table],
        axis=-1,
    )


def token_layout(group_lengths, first_place, row_count):
    ends = jnp.cumsum(group_lengths)
    starts = ends - group_lengths
    places = first_place + jnp.arange(row_count, dtype=jnp.int32)
    member = jnp.sum((places[:, None] >= ends[None, :]).astype(jnp.int32), axis=1)
    chosen = member[:, None] == jnp.arange(group_lengths.shape[0], dtype=jnp.int32)[None, :]
    offsets = jnp.sum(jnp.where(chosen, starts[None, :], 0), axis=1)
    return (member, places, places - offsets)


def make_queries(normed, positions, query_weight, latent_down, latent_gain, key_absorb):
    row_count = normed.shape[0]
    head_count = key_absorb.shape[0]
    plain_width = key_absorb.shape[1]
    latent_width = latent_gain.shape[0]
    projected = lax.optimization_barrier(
        jnp.dot(normed, query_weight, preferred_element_type=jnp.float32)
    ).reshape(row_count, head_count, -1)
    rope_width = projected.shape[-1] - plain_width
    cosine, sine_table = rope_tables(positions, rope_width)
    query_plain = projected[..., :plain_width].astype(jnp.bfloat16)
    query_rotary = rotate(
        projected[..., plain_width:], cosine[:, None, :], sine_table[:, None, :]
    ).astype(jnp.bfloat16)
    query_latent = jnp.einsum(
        "thn,hnr->thr", query_plain, key_absorb, preferred_element_type=jnp.float32
    ).astype(jnp.bfloat16)
    query_rows = jnp.concatenate([query_latent, query_rotary], axis=-1)
    compressed = jnp.dot(normed, latent_down, preferred_element_type=jnp.float32)
    latent = rms_scale(compressed[:, :latent_width], latent_gain)
    key_rotary = rotate(compressed[:, latent_width:], cosine, sine_table)
    key_rows = jnp.concatenate([latent, key_rotary], axis=-1).astype(jnp.bfloat16)
    return (query_rows, key_rows)


def attend_block(state_now, query_rows, key_block, visible, scale_factor, latent_width):
    running_max, running_sum, weighted_sum = state_now
    scores = (
        lax.dot_general(
            query_rows, key_block, (((1,), (1,)), ((), ())), preferred_element_type=jnp.float32
        )
        * scale_factor
    )
    scores = jnp.where(visible, scores, -jnp.inf)
    new_max = jnp.maximum(running_max, jnp.max(scores, axis=1))
    rescale = jnp.exp(running_max - new_max)
    weights = jnp.exp(scores - new_max[:, None])
    running_sum = running_sum * rescale + jnp.sum(weights, axis=1)
    weighted_sum = weighted_sum * rescale[:, None] + jnp.dot(
        weights.astype(jnp.bfloat16),
        key_block[:, :latent_width],
        preferred_element_type=jnp.float32,
    )
    return (new_max, running_sum, weighted_sum)


def expert_apply(token_rows, expert_gate_up, expert_down):
    hidden_units = expert_down.shape[1]
    rows = token_rows.reshape(-1, token_rows.shape[-1])
    joint = jnp.dot(rows, expert_gate_up[0], preferred_element_type=jnp.float32)
    active = (jax.nn.silu(joint[:, :hidden_units]) * joint[:, hidden_units:]).astype(jnp.bfloat16)
    produced = jnp.dot(active, expert_down[0], preferred_element_type=jnp.float32)
    return produced.astype(jnp.bfloat16).reshape(token_rows.shape)


def gather_rows(rows, axes):
    count = lax.axis_size(axes)
    copies = jnp.broadcast_to(rows[None], (count,) + rows.shape)
    gathered = lax.all_to_all(copies, axes, split_axis=0, concat_axis=0, tiled=True)
    return gathered.reshape(count * rows.shape[0], rows.shape[1])


def ring_gather(rows, axis):
    size = lax.axis_size(axis)
    own = lax.axis_index(axis)
    pieces = [rows]
    for shift in range(1, size):
        pairs = [(i, (i + shift) % size) for i in range(size)]
        pieces.append(lax.ppermute(rows, axis, pairs))
    sources = (own - jnp.arange(size, dtype=jnp.int32)) % size
    return jnp.concatenate(pieces, axis=0), sources


def on_device(
    hidden,
    lengths,
    prefix_latent,
    gain_in,
    query_weight,
    latent_down,
    latent_gain,
    key_absorb,
    value_up,
    output_weight,
    post_gain,
    routes,
    gate_weights,
    expert_gate_up,
    expert_down,
):
    token_count = hidden.shape[1]
    model_width = hidden.shape[2]
    head_count = key_absorb.shape[0]
    latent_width = latent_gain.shape[0]
    scale_factor = float(query_weight.shape[1] // head_count) ** (-0.5)
    group_lengths = lengths[0]
    prefix_total = prefix_latent.shape[0] * lax.axis_size(("row", "col", "rep"))
    first_place = lax.axis_index(("row", "col")) * token_count
    member, places, offsets = token_layout(group_lengths, first_place, token_count)
    own_tokens = hidden[0]
    normed = rms_scale(own_tokens.astype(jnp.float32), gain_in).astype(jnp.bfloat16)
    query_rows, key_rows = make_queries(
        normed, prefix_total + offsets, query_weight, latent_down, latent_gain, key_absorb
    )
    query_rows = query_rows.reshape(token_count * head_count, -1)
    row_member = jnp.repeat(member, head_count)
    row_places = jnp.repeat(places, head_count)
    row_total = token_count * head_count
    initial = (
        jnp.full((row_total,), floor_value, jnp.float32),
        jnp.zeros((row_total,), jnp.float32),
        jnp.zeros((row_total, latent_width), jnp.float32),
    )
    after_prefix = attend_block(
        initial,
        query_rows,
        gather_rows(prefix_latent, ("row", "col", "rep")),
        True,
        scale_factor,
        latent_width,
    )
    key_block, col_sources = ring_gather(key_rows, "col")
    key_block, row_sources = ring_gather(key_block, "row")
    source_devices = row_sources[:, None] * lax.axis_size("col") + col_sources[None, :]
    block_places = (
        source_devices.reshape(-1)[:, None] * token_count
        + jnp.arange(token_count, dtype=jnp.int32)[None, :]
    ).reshape(-1)
    block_member = jnp.sum(
        (block_places[:, None] >= jnp.cumsum(group_lengths)[None, :]).astype(jnp.int32), axis=1
    )
    visible = (row_member[:, None] == block_member[None, :]) & (
        row_places[:, None] >= block_places[None, :]
    )
    final_state = attend_block(
        after_prefix, query_rows, key_block, visible, scale_factor, latent_width
    )
    running_max, running_sum, weighted_sum = final_state
    mixed = (
        (weighted_sum / running_sum[:, None])
        .astype(jnp.bfloat16)
        .reshape(token_count, head_count, latent_width)
    )
    head_values = (
        jnp.einsum("thr,hrv->thv", mixed, value_up, preferred_element_type=jnp.float32)
        .astype(jnp.bfloat16)
        .reshape(token_count, -1)
    )
    attention = jnp.dot(head_values, output_weight, preferred_element_type=jnp.float32)
    residual = (own_tokens.astype(jnp.float32) + attention).astype(jnp.bfloat16)
    normed_post = rms_scale(residual.astype(jnp.float32), post_gain).astype(jnp.bfloat16)
    top_count = routes.shape[2]
    pair_count = token_count * top_count
    choices_flat = routes[0].reshape(-1)
    selected = (choices_flat[:, None] == jnp.arange(E, dtype=jnp.int32)[None, :]).astype(
        jnp.bfloat16
    )
    pair_ids = jnp.arange(pair_count, dtype=jnp.int32)
    lower = (pair_ids[:, None] >= pair_ids[None, :]).astype(jnp.bfloat16)
    running = jnp.dot(lower, selected, preferred_element_type=jnp.float32)
    slot_index = (
        jnp.sum(running * selected.astype(jnp.float32), axis=1).astype(jnp.int32) - 1
    )
    slot_place = choices_flat * CAP + slot_index
    pick_table = (
        slot_place[:, None] == jnp.arange(E * CAP, dtype=jnp.int32)[None, :]
    ).astype(jnp.bfloat16).reshape(token_count, top_count, E * CAP)
    occupancy = jnp.sum(pick_table, axis=1).reshape(token_count, E, 1, CAP)
    send_table = jnp.broadcast_to(occupancy, (token_count, E, 2, CAP))
    pick_slots = pick_table.reshape(token_count, top_count, E, CAP)
    device_count = lax.axis_size(("row", "col", "rep"))
    per_device = expert_gate_up.shape[0]
    chunk_count = 2
    chunk = CAP // chunk_count
    gate_table = jnp.sum(
        pick_slots.astype(jnp.float32) * gate_weights[0][:, :, None, None], axis=1
    )
    mixture = None
    for part in range(chunk_count):
        window = slice(part * chunk, (part + 1) * chunk)
        outgoing = (
            jnp.einsum(
                "tj,td->jd",
                send_table[..., window].reshape(token_count, -1),
                normed_post,
                preferred_element_type=jnp.float32,
            )
            .astype(jnp.bfloat16)
            .reshape(device_count, per_device, chunk, model_width)
        )
        produced = expert_apply(
            lax.all_to_all(
                outgoing, ("row", "col", "rep"), split_axis=0, concat_axis=0, tiled=True
            ),
            expert_gate_up,
            expert_down,
        )
        returned = lax.all_to_all(
            produced, ("row", "col", "rep"), split_axis=0, concat_axis=0, tiled=True
        ).reshape(E, 2, chunk, model_width)
        paired = returned[:, 0].astype(jnp.float32) + returned[:, 1].astype(jnp.float32)
        term = jnp.dot(
            gate_table[..., window].reshape(token_count, E * chunk),
            paired.reshape(E * chunk, model_width),
            precision=lax.Precision.HIGHEST,
            preferred_element_type=jnp.float32,
        )
        mixture = term if mixture is None else mixture + term
    layer_out = (residual.astype(jnp.float32) + mixture).astype(jnp.bfloat16)
    return (attention.astype(jnp.bfloat16)[None], layer_out[None])


def solution(mesh):
    in_specs = (
        P("rep", ("row", "col"), None),
        P("rep", None),
        P(("row", "col", "rep"), None),
        P(),
        P(),
        P(),
        P(),
        P(),
        P(),
        P(),
        P(),
        P("rep", ("row", "col"), None),
        P("rep", ("row", "col"), None),
        P(("row", "col", "rep"), None, None),
        P(("row", "col", "rep"), None, None),
    )
    out_specs = (P("rep", ("row", "col"), None), P("rep", ("row", "col"), None))
    return jax.shard_map(
        on_device, mesh=mesh, in_specs=in_specs, out_specs=out_specs, check_vma=False
    )
```
